256 devices in a mesh: rows: 128 (over x, y, z), help: 2 (over core).
Axes of the slice: x: 4, y: 4, z: 8, core: 2. Of those that a mesh axis runs over, the one named last changes fastest.
Arguments:
- density: float32 [256, 5, 256, 256], P('rows', None, None, 'help'), as said below
- pattern: int32 [256, 5], P('rows'), may hold values from 0 to 1, as said below
- truncation: int32 [2, 256, 5], P(None, 'rows'), may hold values from 0 to 1, as said below
Outputs:
- purified: float32 [256, 5, 256, 256], P('rows', None, None, 'help')
The draws below stay inside these ranges and needn't reach their ends.
Inputs may be any that keep to these rules, and one draw needn't show every extreme that they name: pattern[i, 2] = 1; pattern[i, s] = pattern[i + s - 2, 4 - s]; pattern[i, s] = 0 where i + s - 2 lies outside 0 to 255. truncation[t] obeys the same three rules as pattern for every t. density is symmetric: tile slot s of block row i is the transpose of slot 4 - s of block row i + s - 2 wherever both lie inside the matrix.
All inputs are finite; a program needn't handle non-finite values.
Results may differ from the reference program's by a relative error of at most 0.0002.
Values sent between devices are 32-bit elements; how exact they have to be, the bound alone decides.
No kernel may reach another device: no remote copies, remote signals or barrier semaphores. Data moves between devices by JAX's collectives and lax.ppermute only.
A program may use at most 64 MiB of HBM per device.

```python
import math
import jax
import jax.numpy as jnp
from jax import lax

B = 256
W = 2
NB = 5
STEPS = 2
NR = 256


def band_mask(key, leading):
    bits = (jax.random.randint(key, (leading, NR, NB), 0, 4) < 3).astype(jnp.int32)
    mirror_list = []
    for slot_index in range(NB):
        mirror_list.append(jnp.roll(bits[:, :, NB - 1 - slot_index], -(slot_index - W), axis=1))
    mirrored = jnp.stack(mirror_list, axis=2)
    slot_grid = jnp.arange(NB)[None, None, :]
    row_grid = jnp.arange(NR)[None, :, None]
    symmetric = jnp.where(slot_grid > W, bits, jnp.where(slot_grid == W, 1, mirrored))
    target = row_grid + slot_grid - W
    inside = (target >= 0) & (target < NR)
    return jnp.where(inside, symmetric, 0).astype(jnp.int32)


def draw_pattern(key, part):
    return band_mask(jax.random.fold_in(key, 11), 1)[0]


def draw_truncation(key, part):
    return band_mask(jax.random.fold_in(key, 23), STEPS)


def draw_density(key, part):
    sigma = 0.7 / math.sqrt(NB * B)
    raw = jax.random.normal(key, (NR, NB, B, B), jnp.float32) * sigma
    mirror_list = []
    for slot_index in range(NB):
        moved = jnp.roll(raw[:, NB - 1 - slot_index], -(slot_index - W), axis=0)
        mirror_list.append(jnp.swapaxes(moved, 1, 2))
    mirrored = jnp.stack(mirror_list, axis=1)
    symmetric = (raw + mirrored) * 0.70710678
    diagonal = jnp.eye(B, dtype=jnp.float32) * 0.5
    slot_pick = (jnp.arange(NB) == W).astype(jnp.float32)
    return (symmetric + slot_pick[None, :, None, None] * diagonal[None, None, :, :]).astype(jnp.float32)


def setup_inputs(seed: int = 0) -> dict:
    arg_keys = jax.random.split(jax.random.key(seed), 4)
    return {
        "density": draw_density(jax.random.fold_in(arg_keys[3], 71), 0),
        "pattern": draw_pattern(jax.random.fold_in(arg_keys[3], 71), 0),
        "truncation": draw_truncation(jax.random.fold_in(arg_keys[3], 71), 0),
    }


def band_square(matrix):
    slot_count = matrix.shape[1]
    band_reach = (slot_count - 1) // 2
    row_count = matrix.shape[0]
    padded = jnp.pad(matrix, ((band_reach, band_reach), (0, 0), (0, 0), (0, 0)))
    running = jnp.zeros_like(matrix)
    for offset_k in range(-band_reach, band_reach + 1):
        left_tile = matrix[:, offset_k + band_reach]
        right_slab = padded[band_reach + offset_k:band_reach + offset_k + row_count]
        low_slot = max(0, -offset_k)
        high_slot = min(slot_count, slot_count - offset_k)
        product_term = jnp.einsum("rab,rtbc->rtac", left_tile, right_slab[:, low_slot:high_slot], precision=lax.Precision.HIGHEST)
        running = running.at[:, low_slot + offset_k:high_slot + offset_k].add(product_term)
    return running


def reference(density, pattern, truncation):
    matrix = density * pattern[:, :, None, None].astype(jnp.float32)
    for step_index in range(STEPS):
        squared = band_square(matrix)
        if step_index % 2 == 0:
            stepped = squared
        else:
            stepped = 2.0 * matrix - squared
        matrix = stepped * truncation[step_index][:, :, None, None].astype(jnp.float32)
    return matrix
```

```python
import jax
import jax.numpy as jnp
from jax import lax
from jax.sharding import PartitionSpec as P

STEPS = 2


def swap_help(value):
    return lax.ppermute(value, "help", [(0, 1), (1, 0)])


def halo_rows(matrix, full):
    count = lax.axis_size("rows")
    half = matrix.shape[3]
    side = lax.axis_index("help")
    block = jnp.stack([matrix[0, 2], matrix[0, 3], matrix[1, 1], matrix[1, 2]])
    from_left = lax.ppermute(block, "rows", [(i, i + 1) for i in range(count - 1)])
    from_right = lax.ppermute(block, "rows", [(i + 1, i) for i in range(count - 1)])
    own_half = lax.dynamic_slice_in_dim(full, side * half, half, axis=2)
    flipped = jnp.swapaxes(own_half, 2, 3)
    zero = jnp.zeros_like(matrix[0, 0])
    left = jnp.stack(
        [
            jnp.stack([zero, zero, from_left[0], from_left[1], flipped[0, 0]]),
            jnp.stack([zero, from_left[2], from_left[3], flipped[0, 1], flipped[1, 0]]),
        ]
    )
    right = jnp.stack(
        [
            jnp.stack([flipped[0, 4], flipped[1, 3], from_right[0], from_right[1], zero]),
            jnp.stack([flipped[1, 4], from_right[2], from_right[3], zero, zero]),
        ]
    )
    return jnp.concatenate([left, matrix, right], axis=0)


def band_square(matrix):
    row_count, slot_count, tile_rows, half_cols = matrix.shape
    band_reach = (slot_count - 1) // 2
    other = swap_help(matrix)
    side = lax.axis_index("help")
    columns = jnp.where(
        side == 0,
        jnp.concatenate([matrix, other], axis=3),
        jnp.concatenate([other, matrix], axis=3),
    )
    extended = halo_rows(matrix, columns)
    result = jnp.zeros_like(matrix)
    for offset_k in range(-band_reach, band_reach + 1):
        left_tile = columns[:, offset_k + band_reach]
        right_slab = extended[band_reach + offset_k : band_reach + offset_k + row_count]
        low_slot = max(0, -offset_k)
        high_slot = min(slot_count, slot_count - offset_k)
        product_term = jnp.einsum(
            "rab,rtbc->rtac",
            left_tile,
            right_slab[:, low_slot:high_slot],
            precision=lax.Precision.HIGHEST,
        )
        result = result.at[:, low_slot + offset_k : high_slot + offset_k].add(product_term)
    return result


def local(density, pattern, truncation):
    matrix = density * pattern[:, :, None, None].astype(jnp.float32)
    for step_index in range(STEPS):
        squared = band_square(matrix)
        if step_index % 2 == 0:
            stepped = squared
        else:
            stepped = 2.0 * matrix - squared
        matrix = stepped * truncation[step_index][:, :, None, None].astype(jnp.float32)
    return matrix


def solution(mesh):
    return jax.shard_map(
        local,
        mesh=mesh,
        in_specs=(P("rows", None, None, "help"), P("rows", None), P(None, "rows", None)),
        out_specs=P("rows", None, None, "help"),
        check_vma=False,
    )
```

```python
import jax
import jax.numpy as jnp
from jax import lax
from jax.sharding import PartitionSpec as P

STEPS = 2
DIAG = ((2, 3), (1, 2))
OFF = ((0, 1, 4), (0, 3, 4))
BLOCK = ((0, 2), (0, 3), (1, 1), (1, 2))


def swap_help(value):
    return lax.ppermute(value, "help", [(0, 1), (1, 0)])


def send_block(block):
    count = lax.axis_size("rows")
    from_left = lax.ppermute(block, "rows", [(i, i + 1) for i in range(count - 1)])
    from_right = lax.ppermute(block, "rows", [(i + 1, i) for i in range(count - 1)])
    return from_left, from_right


def full_tiles(matrix):
    half = matrix.shape[3]
    side = lax.axis_index("help")
    other = swap_help(matrix)
    full = jnp.where(
        side == 0,
        jnp.concatenate([matrix, other], axis=3),
        jnp.concatenate([other, matrix], axis=3),
    )
    own_half = lax.dynamic_slice_in_dim(full, side * half, half, axis=2)
    return full, jnp.swapaxes(own_half, 2, 3)


def right_tile(k, j, matrix, flipped, from_left, from_right):
    if abs(k - j) > 2:
        return None
    if k in (0, 1):
        return matrix[k, j - k + 2]
    if j in (0, 1):
        return flipped[j, k - j + 2]
    if k < 0:
        return from_left[2 * (k + 2) + (j + 2)]
    return from_right[2 * (k - 2) + (j - 2)]


def products(full, matrix, flipped, from_left, from_right, slots):
    zero = jnp.zeros_like(matrix[0, 0])
    rows = []
    for row, row_slots in enumerate(slots):
        by_k = []
        for offset in range(5):
            k = row + offset - 2
            tiles = []
            for slot in row_slots:
                tile = right_tile(k, row + slot - 2, matrix, flipped, from_left, from_right)
                tiles.append(zero if tile is None else tile)
            by_k.append(jnp.concatenate(tiles, axis=1))
        rows.append(jnp.stack(by_k))
    right = jnp.stack(rows)
    out = jnp.einsum("asxy,asyn->axn", full, right, precision=lax.Precision.HIGHEST)
    half = matrix.shape[3]
    return [
        [out[row, :, n * half : (n + 1) * half] for n in range(len(row_slots))]
        for row, row_slots in enumerate(slots)
    ]


def assemble(diag, off):
    tiles = {}
    for row in range(2):
        for slot, tile in zip(DIAG[row], diag[row]):
            tiles[(row, slot)] = tile
        for slot, tile in zip(OFF[row], off[row]):
            tiles[(row, slot)] = tile
    return jnp.stack([jnp.stack([tiles[(row, slot)] for slot in range(5)]) for row in range(2)])


def local(density, pattern, truncation):
    keep = [truncation[t].astype(jnp.float32) for t in range(STEPS)]
    matrix = density * pattern[:, :, None, None].astype(jnp.float32)
    block = jnp.stack([matrix[row, slot] for row, slot in BLOCK])
    halo = send_block(block)
    for step_index in range(STEPS):
        full, flipped = full_tiles(matrix)
        diag = products(full, matrix, flipped, None, None, DIAG)
        if step_index % 2 == 1:
            diag = [[2.0 * matrix[row, slot] - tile for slot, tile in zip(DIAG[row], diag[row])] for row in range(2)]
        diag = [[tile * keep[step_index][row, slot] for slot, tile in zip(DIAG[row], diag[row])] for row in range(2)]
        if step_index + 1 < STEPS:
            next_block = jnp.stack([diag[0][0], diag[0][1], diag[1][0], diag[1][1]])
            next_halo = send_block(next_block)
        off = products(full, matrix, flipped, halo[0], halo[1], OFF)
        if step_index % 2 == 1:
            off = [[2.0 * matrix[row, slot] - tile for slot, tile in zip(OFF[row], off[row])] for row in range(2)]
        off = [[tile * keep[step_index][row, slot] for slot, tile in zip(OFF[row], off[row])] for row in range(2)]
        matrix = assemble(diag, off)
        if step_index + 1 < STEPS:
            halo = next_halo
    return matrix


def solution(mesh):
    return jax.shard_map(
        local,
        mesh=mesh,
        in_specs=(P("rows", None, None, "help"), P("rows", None), P(None, "rows", None)),
        out_specs=P("rows", None, None, "help"),
        check_vma=False,
    )
```

```python
import functools

import jax
import jax.numpy as jnp
from jax import lax
from jax.experimental import pallas as pl
from jax.experimental.pallas import tpu as pltpu
from jax.sharding import PartitionSpec as P


STEPS = 2
DIAG = ((0, 2), (0, 3), (1, 1), (1, 2))
OFF = ((0, 0), (0, 1), (0, 4), (1, 0), (1, 3), (1, 4))
CONTRACT = (((1,), (0,)), ((), ()))
CONTRACT_T = (((1,), (1,)), ((), ()))


def swap_help(value):
    return lax.ppermute(value, "help", [(0, 1), (1, 0)])


def send_block(block):
    count = lax.axis_size("rows")
    from_left = lax.ppermute(block, "rows", [(i, i + 1) for i in range(count - 1)])
    from_right = lax.ppermute(block, "rows", [(i + 1, i) for i in range(count - 1)])
    return from_left, from_right


def dot(a, b, dims):
    return lax.dot_general(a, b, dims, precision=lax.Precision.HIGHEST, preferred_element_type=jnp.float32)


def band_kernel(tiles, odd, side_ref, keep_ref, mine_ref, other_ref, *rest):
    if len(rest) == 3:
        left_ref, right_ref, out_ref = rest
    else:
        left_ref = right_ref = None
        (out_ref,) = rest
    half = mine_ref.shape[3]
    side = side_ref[0]
    own = pl.ds(pl.multiple_of(side * half, half), half)
    far = pl.ds(pl.multiple_of((1 - side) * half, half), half)
    for index, (row, slot) in enumerate(tiles):
        col = row + slot - 2
        acc = jnp.zeros(out_ref.shape[1:], jnp.float32)
        for k in range(max(row, col) - 2, min(row, col) + 3):
            lm = mine_ref[row, k - row + 2]
            lo = other_ref[row, k - row + 2]
            if k in (0, 1) or col not in (0, 1):
                if k in (0, 1):
                    src, a, b = mine_ref, k, col - k + 2
                elif k < 0:
                    src, a, b = left_ref, 0, 2 * (k + 2) + (col + 2)
                else:
                    src, a, b = right_ref, 0, 2 * (k - 2) + (col - 2)
                if src is mine_ref:
                    r_own = src[a, b, own, :]
                    r_far = src[a, b, far, :]
                else:
                    r_own = src[b, own, :]
                    r_far = src[b, far, :]
                acc += dot(lm, r_own, CONTRACT) + dot(lo, r_far, CONTRACT)
            else:
                s = k - col + 2
                acc += dot(lm, mine_ref[col, s, own, :], CONTRACT_T)
                acc += dot(lo, other_ref[col, s, own, :], CONTRACT_T)
        if odd:
            acc = 2.0 * mine_ref[row, slot] - acc
        out_ref[index] = acc * keep_ref[row, slot]


def band_call(tiles, odd, side, keep, mine, other, halo=None):
    smem = pl.BlockSpec(memory_space=pltpu.SMEM)
    vmem = pl.BlockSpec(memory_space=pltpu.VMEM)
    args = [side, keep, mine, other] + ([] if halo is None else list(halo))
    return pl.pallas_call(
        functools.partial(band_kernel, tiles, odd),
        out_shape=jax.ShapeDtypeStruct((len(tiles),) + mine.shape[2:], jnp.float32),
        in_specs=[smem, smem] + [vmem] * (len(args) - 2),
        out_specs=vmem,
    )(*args)


def assemble(diag, off):
    tiles = {}
    for index, key in enumerate(DIAG):
        tiles[key] = diag[index]
    for index, key in enumerate(OFF):
        tiles[key] = off[index]
    return jnp.stack([jnp.stack([tiles[(row, slot)] for slot in range(5)]) for row in range(2)])


def purify(density, pattern, truncation):
    side = lax.axis_index("help").astype(jnp.int32).reshape(1)
    matrix = density * pattern[:, :, None, None].astype(jnp.float32)
    halo = send_block(jnp.stack([matrix[row, slot] for row, slot in DIAG]))
    for step_index in range(STEPS):
        keep = truncation[step_index].astype(jnp.float32)
        odd = step_index % 2 == 1
        other = swap_help(matrix)
        diag = band_call(DIAG, odd, side, keep, matrix, other)
        if step_index + 1 < STEPS:
            next_halo = send_block(diag)
        off = band_call(OFF, odd, side, keep, matrix, other, halo)
        matrix = assemble(diag, off)
        if step_index + 1 < STEPS:
            halo = next_halo
    return matrix


def solution(mesh):
    return jax.shard_map(
        purify,
        mesh=mesh,
        in_specs=(P("rows", None, None, "help"), P("rows", None), P(None, "rows", None)),
        out_specs=P("rows", None, None, "help"),
        check_vma=False,
    )
```

```python
import functools

import jax
import jax.numpy as jnp
from jax import lax
from jax.experimental import pallas as pl
from jax.experimental.pallas import tpu as pltpu
from jax.sharding import PartitionSpec as P


STEPS = 2
DIAG = ((0, 2), (0, 3), (1, 1), (1, 2))
OFF = ((0, 0), (0, 1), (0, 4), (1, 0), (1, 3), (1, 4))
CONTRACT = (((1,), (0,)), ((), ()))
CONTRACT_T = (((1,), (1,)), ((), ()))


def swap_help(value):
    return lax.ppermute(value, "help", [(0, 1), (1, 0)])


def send_block(block):
    count = lax.axis_size("rows")
    from_left = lax.ppermute(block, "rows", [(i, i + 1) for i in range(count - 1)])
    from_right = lax.ppermute(block, "rows", [(i + 1, i) for i in range(count - 1)])
    return from_left, from_right


def split(x):
    high = x.astype(jnp.bfloat16)
    return high, (x - high.astype(jnp.float32)).astype(jnp.bfloat16)


def dot3(a_high, a_low, b, dims):
    b_high, b_low = split(b)

    def one(x, y):
        return lax.dot_general(x, y, dims, preferred_element_type=jnp.float32)

    return one(a_low, b_high) + one(a_high, b_low) + one(a_high, b_high)


def band_kernel(tiles, odd, side_ref, scale_ref, keep_ref, mine_ref, other_ref, *rest):
    if len(rest) == 6:
        left_ref, right_ref, diag_ref, out_ref, high_ref, low_ref = rest
    else:
        left_ref = right_ref = diag_ref = None
        out_ref, high_ref, low_ref = rest
    half = mine_ref.shape[3]
    side = side_ref[0]
    own = pl.ds(pl.multiple_of(side * half, half), half)
    far = pl.ds(pl.multiple_of((1 - side) * half, half), half)

    def scale(row, slot):
        return scale_ref[row, slot].astype(jnp.float32)

    for row in range(2):
        for slot in range(5):
            full = jnp.concatenate([mine_ref[row, slot], other_ref[row, slot]], axis=1) * scale(row, slot)
            high, low = split(full)
            high_ref[row, slot] = high
            low_ref[row, slot] = low
    for index, (row, slot) in enumerate(tiles):
        col = row + slot - 2
        acc = jnp.zeros(mine_ref.shape[2:], jnp.float32)
        for k in range(max(row, col) - 2, min(row, col) + 3):
            a_high = high_ref[row, k - row + 2]
            a_low = low_ref[row, k - row + 2]
            if k in (0, 1):
                b = col - k + 2
                right = jnp.concatenate([mine_ref[k, b, own, :], mine_ref[k, b, far, :]], axis=0) * scale(k, b)
                acc += dot3(a_high, a_low, right, CONTRACT)
            elif col not in (0, 1):
                src = left_ref if k < 0 else right_ref
                b = 2 * (k + 2) + (col + 2) if k < 0 else 2 * (k - 2) + (col - 2)
                right = jnp.concatenate([src[b, own, :], src[b, far, :]], axis=0)
                acc += dot3(a_high, a_low, right, CONTRACT)
            else:
                s = k - col + 2
                flipped = jnp.concatenate([mine_ref[col, s, own, :], other_ref[col, s, own, :]], axis=1) * scale(col, s)
                acc += dot3(a_high, a_low, flipped, CONTRACT_T)
        if odd:
            acc = 2.0 * mine_ref[row, slot] * scale(row, slot) - acc
        value = acc * keep_ref[row, slot].astype(jnp.float32)
        if diag_ref is None:
            out_ref[index] = value
        else:
            out_ref[row, slot] = value
    if diag_ref is not None:
        for index, (row, slot) in enumerate(DIAG):
            out_ref[row, slot] = diag_ref[index]


def band_call(tiles, odd, side, scale, keep, mine, other, halo=None, diag=None):
    smem = pl.BlockSpec(memory_space=pltpu.SMEM)
    vmem = pl.BlockSpec(memory_space=pltpu.VMEM)
    args = [side, scale, keep, mine, other]
    if halo is None:
        shape = (len(tiles),) + mine.shape[2:]
    else:
        args += [halo[0], halo[1], diag]
        shape = mine.shape
    full = mine.shape[:2] + (mine.shape[2], 2 * mine.shape[3])
    return pl.pallas_call(
        functools.partial(band_kernel, tiles, odd),
        out_shape=jax.ShapeDtypeStruct(shape, jnp.float32),
        in_specs=[smem, smem, smem] + [vmem] * (len(args) - 3),
        out_specs=vmem,
        scratch_shapes=[pltpu.VMEM(full, jnp.bfloat16), pltpu.VMEM(full, jnp.bfloat16)],
    )(*args)


def purify(density, pattern, truncation):
    side = lax.axis_index("help").astype(jnp.int32).reshape(1)
    block = jnp.stack([density[row, slot] * pattern[row, slot].astype(jnp.float32) for row, slot in DIAG])
    halo = send_block(block)
    matrix = density
    scale = pattern
    for step_index in range(STEPS):
        keep = truncation[step_index]
        odd = step_index % 2 == 1
        other = swap_help(matrix)
        diag = band_call(DIAG, odd, side, scale, keep, matrix, other)
        if step_index + 1 < STEPS:
            next_halo = send_block(diag)
        matrix = band_call(OFF, odd, side, scale, keep, matrix, other, halo, diag)
        scale = jnp.ones_like(pattern)
        if step_index + 1 < STEPS:
            halo = next_halo
    return matrix


def solution(mesh):
    return jax.shard_map(
        purify,
        mesh=mesh,
        in_specs=(P("rows", None, None, "help"), P("rows", None), P(None, "rows", None)),
        out_specs=P("rows", None, None, "help"),
        check_vma=False,
    )
```

```python
import functools

import jax
import jax.numpy as jnp
from jax import lax
from jax.experimental import pallas as pl
from jax.experimental.pallas import tpu as pltpu
from jax.sharding import PartitionSpec as P


DIAG = ((0, 2), (0, 3), (1, 1), (1, 2))
OFF = ((0, 0), (0, 1), (0, 4), (1, 0), (1, 3), (1, 4))
ALL = tuple((row, slot) for row in range(2) for slot in range(5))
CONTRACT = (((1,), (0,)), ((), ()))
CONTRACT_T = (((1,), (1,)), ((), ()))


def swap_help(value):
    return lax.ppermute(value, "help", [(0, 1), (1, 0)])


def send_block(block):
    count = lax.axis_size("rows")
    from_left = lax.ppermute(block, "rows", [(i, i + 1) for i in range(count - 1)])
    from_right = lax.ppermute(block, "rows", [(i + 1, i) for i in range(count - 1)])
    return from_left, from_right


def split(x):
    high = x.astype(jnp.bfloat16)
    return high, (x - high.astype(jnp.float32)).astype(jnp.bfloat16)


def dot3(a_high, a_low, b, dims):
    b_high, b_low = split(b)
    def one(x, y):
        return lax.dot_general(x, y, dims, preferred_element_type=jnp.float32)
    return one(a_low, b_high) + one(a_high, b_low) + one(a_high, b_high)


class Tiles:
    def __init__(self, refs, scale):
        self.refs = refs
        self.scale = scale

    def __call__(self, row, slot, rows=slice(None)):
        if len(self.refs) == 1:
            value = self.refs[0][row, slot, rows, :]
        elif (row, slot) in DIAG:
            value = self.refs[0][DIAG.index((row, slot)), rows, :]
        else:
            value = self.refs[1][OFF.index((row, slot)), rows, :]
        if self.scale is not None:
            value = value * self.scale[row, slot].astype(jnp.float32)
        return value


def band_kernel(tiles, odd, parts, scaled, halo, side_ref, scale_ref, keep_ref, *rest):
    mine = Tiles(rest[:parts], scale_ref if scaled else None)
    other = Tiles(rest[parts : 2 * parts], scale_ref if scaled else None)
    rest = rest[2 * parts :]
    if halo:
        left_ref, right_ref = rest[:2]
        rest = rest[2:]
    out_ref, high_ref, low_ref = rest
    half = high_ref.shape[3] // 2
    side = side_ref[0]
    own = pl.ds(pl.multiple_of(side * half, half), half)
    far = pl.ds(pl.multiple_of((1 - side) * half, half), half)

    for row in range(2):
        for slot in range(5):
            high, low = split(jnp.concatenate([mine(row, slot), other(row, slot)], axis=1))
            high_ref[row, slot] = high
            low_ref[row, slot] = low
    for index, (row, slot) in enumerate(tiles):
        col = row + slot - 2
        acc = jnp.zeros((high_ref.shape[2], half), jnp.float32)
        for k in range(max(row, col) - 2, min(row, col) + 3):
            a_high = high_ref[row, k - row + 2]
            a_low = low_ref[row, k - row + 2]
            if k in (0, 1):
                b = col - k + 2
                right = jnp.concatenate([mine(k, b, own), mine(k, b, far)], axis=0)
                acc += dot3(a_high, a_low, right, CONTRACT)
            elif col not in (0, 1):
                src = left_ref if k < 0 else right_ref
                b = 2 * (k + 2) + (col + 2) if k < 0 else 2 * (k - 2) + (col - 2)
                right = jnp.concatenate([src[b, own, :], src[b, far, :]], axis=0)
                acc += dot3(a_high, a_low, right, CONTRACT)
            else:
                s = k - col + 2
                flipped = jnp.concatenate([mine(col, s, own), other(col, s, own)], axis=1)
                acc += dot3(a_high, a_low, flipped, CONTRACT_T)
        if odd:
            acc = 2.0 * mine(row, slot) - acc
        value = acc * keep_ref[row, slot].astype(jnp.float32)
        if len(tiles) == len(ALL):
            out_ref[row, slot] = value
        else:
            out_ref[index] = value


def band_call(tiles, odd, side, scale, keep, mine, other, halo=None, scaled=False):
    smem = pl.BlockSpec(memory_space=pltpu.SMEM)
    vmem = pl.BlockSpec(memory_space=pltpu.VMEM)
    args = [side, scale, keep] + list(mine) + list(other) + ([] if halo is None else list(halo))
    half = mine[0].shape[-1]
    tile = (mine[0].shape[-2], half)
    shape = (2, 5) + tile if len(tiles) == len(ALL) else (len(tiles),) + tile
    full = (2, 5, tile[0], 2 * half)
    return pl.pallas_call(
        functools.partial(band_kernel, tiles, odd, len(mine), scaled, halo is not None),
        out_shape=jax.ShapeDtypeStruct(shape, jnp.float32),
        in_specs=[smem, smem, smem] + [vmem] * (len(args) - 3),
        out_specs=vmem,
        scratch_shapes=[pltpu.VMEM(full, jnp.bfloat16), pltpu.VMEM(full, jnp.bfloat16)],
    )(*args)


def block_kernel(pattern_ref, density_ref, out_ref):
    for index, (row, slot) in enumerate(DIAG):
        out_ref[index] = density_ref[row, slot] * pattern_ref[row, slot].astype(jnp.float32)


def first_block(pattern, density):
    return pl.pallas_call(
        block_kernel,
        out_shape=jax.ShapeDtypeStruct((len(DIAG),) + density.shape[2:], jnp.float32),
        in_specs=[pl.BlockSpec(memory_space=pltpu.SMEM), pl.BlockSpec(memory_space=pltpu.VMEM)],
        out_specs=pl.BlockSpec(memory_space=pltpu.VMEM),
    )(pattern, density)


def purify(density, pattern, truncation):
    side = lax.axis_index("help").astype(jnp.int32).reshape(1)
    halo = send_block(first_block(pattern, density))
    other = swap_help(density)
    diag = band_call(DIAG, False, side, pattern, truncation[0], [density], [other], scaled=True)
    next_halo = send_block(diag)
    diag_other = swap_help(diag)
    off = band_call(OFF, False, side, pattern, truncation[0], [density], [other], halo, scaled=True)
    off_other = swap_help(off)
    return band_call(ALL, True, side, pattern, truncation[1], [diag, off], [diag_other, off_other], next_halo)


def solution(mesh):
    return jax.shard_map(
        purify,
        mesh=mesh,
        in_specs=(P("rows", None, None, "help"), P("rows", None), P(None, "rows", None)),
        out_specs=P("rows", None, None, "help"),
        check_vma=False,
    )
```

```python
import functools

import jax
import jax.numpy as jnp
from jax import lax
from jax.experimental import pallas as pl
from jax.experimental.pallas import tpu as pltpu
from jax.sharding import PartitionSpec as P


DIAG = ((0, 2), (0, 3), (1, 1), (1, 2))
OFF = ((0, 0), (0, 1), (0, 4), (1, 0), (1, 3), (1, 4))
ALL = tuple((row, slot) for row in range(2) for slot in range(5))
CONTRACT = (((1,), (0,)), ((), ()))


def swap_help(value):
    return lax.ppermute(value, "help", [(0, 1), (1, 0)])


def send_block(block):
    count = lax.axis_size("rows")
    from_left = lax.ppermute(block, "rows", [(i, i + 1) for i in range(count - 1)])
    from_right = lax.ppermute(block, "rows", [(i + 1, i) for i in range(count - 1)])
    return from_left, from_right


def split(x):
    high = x.astype(jnp.bfloat16)
    return high, (x - high.astype(jnp.float32)).astype(jnp.bfloat16)


class Tiles:
    def __init__(self, refs, scale):
        self.refs = refs
        self.scale = scale

    def __call__(self, row, slot, rows=slice(None)):
        if len(self.refs) == 1:
            value = self.refs[0][row, slot, rows, :]
        elif (row, slot) in DIAG:
            value = self.refs[0][DIAG.index((row, slot)), rows, :]
        else:
            value = self.refs[1][OFF.index((row, slot)), rows, :]
        if self.scale is not None:
            value = value * self.scale[row, slot].astype(jnp.float32)
        return value


def band_kernel(tiles, odd, parts, scaled, halo, side_ref, scale_ref, keep_ref, *rest):
    mine = Tiles(rest[:parts], scale_ref if scaled else None)
    other = Tiles(rest[parts : 2 * parts], scale_ref if scaled else None)
    rest = rest[2 * parts :]
    if halo:
        left_ref, right_ref = rest[:2]
        rest = rest[2:]
    out_ref, lh_ref, ll_ref, rh_ref, rl_ref = rest
    tile = lh_ref.shape[1]
    half = tile // 2
    side = side_ref[0]
    own = pl.ds(pl.multiple_of(side * half, half), half)
    far = pl.ds(pl.multiple_of((1 - side) * half, half), half)
    by_row = [[(index, slot) for index, (row, slot) in enumerate(tiles) if row == r] for r in range(2)]

    for row in range(2):
        for slot in range(5):
            high, low = split(jnp.concatenate([mine(row, slot), other(row, slot)], axis=1))
            lh_ref[row, :, slot * tile : (slot + 1) * tile] = high
            ll_ref[row, :, slot * tile : (slot + 1) * tile] = low
        for offset in range(5):
            k = row + offset - 2
            for place, (index, slot) in enumerate(by_row[row]):
                col = row + slot - 2
                where = (row, slice(offset * tile, (offset + 1) * tile), slice(place * half, (place + 1) * half))
                if abs(k - col) > 2:
                    rh_ref[where] = jnp.zeros((tile, half), jnp.bfloat16)
                    rl_ref[where] = jnp.zeros((tile, half), jnp.bfloat16)
                    continue
                if k in (0, 1):
                    b = col - k + 2
                    right = jnp.concatenate([mine(k, b, own), mine(k, b, far)], axis=0)
                elif col not in (0, 1):
                    src = left_ref if k < 0 else right_ref
                    b = 2 * (k + 2) + (col + 2) if k < 0 else 2 * (k - 2) + (col - 2)
                    right = jnp.concatenate([src[b, own, :], src[b, far, :]], axis=0)
                else:
                    s = k - col + 2
                    right = jnp.concatenate([mine(col, s, own), other(col, s, own)], axis=1).T
                high, low = split(right)
                rh_ref[where] = high
                rl_ref[where] = low
    for row in range(2):
        def one(x, y):
            return lax.dot_general(x, y, CONTRACT, preferred_element_type=jnp.float32)
        a_high = lh_ref[row]
        b_high = rh_ref[row]
        acc = one(ll_ref[row], b_high) + one(a_high, rl_ref[row]) + one(a_high, b_high)
        for place, (index, slot) in enumerate(by_row[row]):
            value = acc[:, place * half : (place + 1) * half]
            if odd:
                value = 2.0 * mine(row, slot) - value
            value = value * keep_ref[row, slot].astype(jnp.float32)
            if len(tiles) == len(ALL):
                out_ref[row, slot] = value
            else:
                out_ref[index] = value


def band_call(tiles, odd, side, scale, keep, mine, other, halo=None, scaled=False):
    smem = pl.BlockSpec(memory_space=pltpu.SMEM)
    vmem = pl.BlockSpec(memory_space=pltpu.VMEM)
    args = [side, scale, keep] + list(mine) + list(other) + ([] if halo is None else list(halo))
    half = mine[0].shape[-1]
    tile = (mine[0].shape[-2], half)
    shape = (2, 5) + tile if len(tiles) == len(ALL) else (len(tiles),) + tile
    width = len(tiles) // 2
    lefts = (2, tile[0], 5 * 2 * half)
    rights = (2, 5 * tile[0], width * half)
    return pl.pallas_call(
        functools.partial(band_kernel, tiles, odd, len(mine), scaled, halo is not None),
        out_shape=jax.ShapeDtypeStruct(shape, jnp.float32),
        in_specs=[smem, smem, smem] + [vmem] * (len(args) - 3),
        out_specs=vmem,
        scratch_shapes=[pltpu.VMEM(lefts, jnp.bfloat16)] * 2 + [pltpu.VMEM(rights, jnp.bfloat16)] * 2,
    )(*args)


def block_kernel(pattern_ref, density_ref, out_ref):
    for index, (row, slot) in enumerate(DIAG):
        out_ref[index] = density_ref[row, slot] * pattern_ref[row, slot].astype(jnp.float32)


def first_block(pattern, density):
    return pl.pallas_call(
        block_kernel,
        out_shape=jax.ShapeDtypeStruct((len(DIAG),) + density.shape[2:], jnp.float32),
        in_specs=[pl.BlockSpec(memory_space=pltpu.SMEM), pl.BlockSpec(memory_space=pltpu.VMEM)],
        out_specs=pl.BlockSpec(memory_space=pltpu.VMEM),
    )(pattern, density)


def purify(density, pattern, truncation):
    side = lax.axis_index("help").astype(jnp.int32).reshape(1)
    halo = send_block(first_block(pattern, density))
    other = swap_help(density)
    diag = band_call(DIAG, False, side, pattern, truncation[0], [density], [other], scaled=True)
    next_halo = send_block(diag)
    diag_other = swap_help(diag)
    off = band_call(OFF, False, side, pattern, truncation[0], [density], [other], halo, scaled=True)
    off_other = swap_help(off)
    return band_call(ALL, True, side, pattern, truncation[1], [diag, off], [diag_other, off_other], next_halo)


def solution(mesh):
    return jax.shard_map(
        purify,
        mesh=mesh,
        in_specs=(P("rows", None, None, "help"), P("rows", None), P(None, "rows", None)),
        out_specs=P("rows", None, None, "help"),
        check_vma=False,
    )
```

```python
import functools

import jax
import jax.numpy as jnp
from jax import lax
from jax.experimental import pallas as pl
from jax.experimental.pallas import tpu as pltpu
from jax.sharding import PartitionSpec as P


DIAG = ((0, 2), (0, 3), (1, 1), (1, 2))
OFF = ((0, 0), (0, 1), (0, 4), (1, 0), (1, 3), (1, 4))
ALL = tuple((row, slot) for row in range(2) for slot in range(5))
CONTRACT = (((1,), (0,)), ((), ()))


def swap_help(value):
    return lax.ppermute(value, "help", [(0, 1), (1, 0)])


def send_block(block):
    count = lax.axis_size("rows")
    from_left = lax.ppermute(block, "rows", [(i, i + 1) for i in range(count - 1)])
    from_right = lax.ppermute(block, "rows", [(i + 1, i) for i in range(count - 1)])
    return from_left, from_right


def split(x):
    high = x.astype(jnp.bfloat16)
    return high, (x - high.astype(jnp.float32)).astype(jnp.bfloat16)


class Tiles:
    def __init__(self, refs, scale):
        self.refs = refs
        self.scale = scale

    def __call__(self, row, slot, rows=slice(None)):
        if len(self.refs) == 1:
            value = self.refs[0][row, slot, rows, :]
        elif (row, slot) in DIAG:
            value = self.refs[0][DIAG.index((row, slot)), rows, :]
        else:
            value = self.refs[1][OFF.index((row, slot)), rows, :]
        if self.scale is not None:
            value = value * self.scale[row, slot].astype(jnp.float32)
        return value


QUARTERS = ((0, 2), (0, 3), (1, 2))
FROM_QUARTER = {(0, 2): (0, False, (0, 2)), (0, 3): (1, False, (1, 1)), (1, 1): (1, True, (0, 3)), (1, 2): (2, False, (1, 2))}


class Rebuilt:
    def __init__(self, quarter_ref, off_ref, mine, side, own, far):
        self.quarter_ref, self.off_ref, self.mine = quarter_ref, off_ref, mine
        self.side, self.own, self.far = side, own, far

    def __call__(self, row, slot, rows=slice(None)):
        if (row, slot) not in DIAG:
            return self.off_ref[OFF.index((row, slot)), rows, :]
        index, flip, source = FROM_QUARTER[(row, slot)]
        quarter = self.quarter_ref[index]
        far_rows = quarter.T if flip else quarter
        own_rows = self.mine(source[0], source[1], self.far).T
        return jnp.where(
            self.side == 0,
            jnp.concatenate([own_rows, far_rows], axis=0),
            jnp.concatenate([far_rows, own_rows], axis=0),
        )


def band_kernel(tiles, odd, parts, scaled, halo, quarters, side_ref, scale_ref, keep_ref, *rest):
    mine = Tiles(rest[:parts], scale_ref if scaled else None)
    other_refs = rest[parts : 2 * parts]
    rest = rest[2 * parts :]
    if halo:
        left_ref, right_ref = rest[:2]
        rest = rest[2:]
    if quarters:
        out_ref, quarter_ref, lh_ref, ll_ref, rh_ref, rl_ref = rest
    else:
        out_ref, lh_ref, ll_ref, rh_ref, rl_ref = rest
    tile = lh_ref.shape[1]
    half = tile // 2
    side = side_ref[0]
    own = pl.ds(pl.multiple_of(side * half, half), half)
    far = pl.ds(pl.multiple_of((1 - side) * half, half), half)
    if other_refs[0].shape[-2] == half:
        other = Rebuilt(other_refs[0], other_refs[1], mine, side, own, far)
    else:
        other = Tiles(other_refs, scale_ref if scaled else None)
    by_row = [[(index, slot) for index, (row, slot) in enumerate(tiles) if row == r] for r in range(2)]

    for row in range(2):
        for slot in range(5):
            high, low = split(jnp.concatenate([mine(row, slot), other(row, slot)], axis=1))
            lh_ref[row, :, slot * tile : (slot + 1) * tile] = high
            ll_ref[row, :, slot * tile : (slot + 1) * tile] = low
        for offset in range(5):
            k = row + offset - 2
            for place, (index, slot) in enumerate(by_row[row]):
                col = row + slot - 2
                where = (row, slice(offset * tile, (offset + 1) * tile), slice(place * half, (place + 1) * half))
                if abs(k - col) > 2:
                    rh_ref[where] = jnp.zeros((tile, half), jnp.bfloat16)
                    rl_ref[where] = jnp.zeros((tile, half), jnp.bfloat16)
                    continue
                if k in (0, 1):
                    b = col - k + 2
                    right = jnp.concatenate([mine(k, b, own), mine(k, b, far)], axis=0)
                elif col not in (0, 1):
                    src = left_ref if k < 0 else right_ref
                    b = 2 * (k + 2) + (col + 2) if k < 0 else 2 * (k - 2) + (col - 2)
                    right = jnp.concatenate([src[b, own, :], src[b, far, :]], axis=0)
                else:
                    s = k - col + 2
                    right = jnp.concatenate([mine(col, s, own), other(col, s, own)], axis=1).T
                high, low = split(right)
                rh_ref[where] = high
                rl_ref[where] = low
    for row in range(2):
        def one(x, y):
            return lax.dot_general(x, y, CONTRACT, preferred_element_type=jnp.float32)

        a_high = lh_ref[row]
        b_high = rh_ref[row]
        acc = one(ll_ref[row], b_high) + one(a_high, rl_ref[row]) + one(a_high, b_high)
        for place, (index, slot) in enumerate(by_row[row]):
            value = acc[:, place * half : (place + 1) * half]
            if odd:
                value = 2.0 * mine(row, slot) - value
            value = value * keep_ref[row, slot].astype(jnp.float32)
            if len(tiles) == len(ALL):
                out_ref[row, slot] = value
            else:
                out_ref[index] = value
    if quarters:
        for index, key in enumerate(QUARTERS):
            quarter_ref[index] = out_ref[tiles.index(key), own, :]


def band_call(tiles, odd, side, scale, keep, mine, other, halo=None, scaled=False, quarters=False):
    smem = pl.BlockSpec(memory_space=pltpu.SMEM)
    vmem = pl.BlockSpec(memory_space=pltpu.VMEM)
    args = [side, scale, keep] + list(mine) + list(other) + ([] if halo is None else list(halo))
    half = mine[0].shape[-1]
    tile = (mine[0].shape[-2], half)
    shape = (2, 5) + tile if len(tiles) == len(ALL) else (len(tiles),) + tile
    width = len(tiles) // 2
    lefts = (2, tile[0], 5 * 2 * half)
    rights = (2, 5 * tile[0], width * half)
    out_shape = jax.ShapeDtypeStruct(shape, jnp.float32)
    if quarters:
        out_shape = (out_shape, jax.ShapeDtypeStruct((len(QUARTERS), half, half), jnp.float32))
    return pl.pallas_call(
        functools.partial(band_kernel, tiles, odd, len(mine), scaled, halo is not None, quarters),
        out_shape=out_shape,
        in_specs=[smem, smem, smem] + [vmem] * (len(args) - 3),
        out_specs=(vmem, vmem) if quarters else vmem,
        scratch_shapes=[pltpu.VMEM(lefts, jnp.bfloat16)] * 2 + [pltpu.VMEM(rights, jnp.bfloat16)] * 2,
    )(*args)


def block_kernel(pattern_ref, density_ref, out_ref):
    for index, (row, slot) in enumerate(DIAG):
        out_ref[index] = density_ref[row, slot] * pattern_ref[row, slot].astype(jnp.float32)


def first_block(pattern, density):
    return pl.pallas_call(
        block_kernel,
        out_shape=jax.ShapeDtypeStruct((len(DIAG),) + density.shape[2:], jnp.float32),
        in_specs=[pl.BlockSpec(memory_space=pltpu.SMEM), pl.BlockSpec(memory_space=pltpu.VMEM)],
        out_specs=pl.BlockSpec(memory_space=pltpu.VMEM),
    )(pattern, density)


def purify(density, pattern, truncation):
    side = lax.axis_index("help").astype(jnp.int32).reshape(1)
    halo = send_block(first_block(pattern, density))
    other = swap_help(density)
    diag, quarter = band_call(DIAG, False, side, pattern, truncation[0], [density], [other], scaled=True, quarters=True)
    next_halo = send_block(diag)
    quarter_other = swap_help(quarter)
    off = band_call(OFF, False, side, pattern, truncation[0], [density], [other], halo, scaled=True)
    off_other = swap_help(off)
    return band_call(ALL, True, side, pattern, truncation[1], [diag, off], [quarter_other, off_other], next_halo)


def solution(mesh):
    return jax.shard_map(
        purify,
        mesh=mesh,
        in_specs=(P("rows", None, None, "help"), P("rows", None), P(None, "rows", None)),
        out_specs=P("rows", None, None, "help"),
        check_vma=False,
    )
```

```python
import functools

import jax
import jax.numpy as jnp
from jax import lax
from jax.experimental import pallas as pl
from jax.experimental.pallas import tpu as pltpu
from jax.sharding import PartitionSpec as P


DIAG = ((0, 2), (0, 3), (1, 1), (1, 2))
OFF = ((0, 0), (0, 1), (0, 4), (1, 0), (1, 3), (1, 4))
ALL = tuple((row, slot) for row in range(2) for slot in range(5))
CONTRACT = (((1,), (0,)), ((), ()))


def swap_help(value):
    return lax.ppermute(value, "help", [(0, 1), (1, 0)])


def send_block(block):
    count = lax.axis_size("rows")
    from_left = lax.ppermute(block, "rows", [(i, i + 1) for i in range(count - 1)])
    from_right = lax.ppermute(block, "rows", [(i + 1, i) for i in range(count - 1)])
    return from_left, from_right


def split(x):
    high = x.astype(jnp.bfloat16)
    return high, (x - high.astype(jnp.float32)).astype(jnp.bfloat16)


def dot3(a_high, a_low, b, dims):
    b_high, b_low = split(b)
    def one(x, y):
        return lax.dot_general(x, y, dims, preferred_element_type=jnp.float32)
    return one(a_low, b_high) + one(a_high, b_low) + one(a_high, b_high)


class Tiles:
    def __init__(self, refs, scale):
        self.refs = refs
        self.scale = scale

    def __call__(self, row, slot, rows=slice(None)):
        if len(self.refs) == 1:
            value = self.refs[0][row, slot, rows, :]
        elif (row, slot) in DIAG:
            value = self.refs[0][DIAG.index((row, slot)), rows, :]
        else:
            value = self.refs[1][OFF.index((row, slot)), rows, :]
        if self.scale is not None:
            value = value * self.scale[row, slot].astype(jnp.float32)
        return value


QUARTERS = ((0, 2), (0, 3), (1, 2))
FROM_QUARTER = {(0, 2): (0, False, (0, 2)), (0, 3): (1, False, (1, 1)), (1, 1): (1, True, (0, 3)), (1, 2): (2, False, (1, 2))}


class Rebuilt:
    def __init__(self, quarter_ref, off_ref, mine, side, own, far):
        self.quarter_ref, self.off_ref, self.mine = quarter_ref, off_ref, mine
        self.side, self.own, self.far = side, own, far

    def __call__(self, row, slot, rows=slice(None)):
        if (row, slot) not in DIAG:
            return self.off_ref[OFF.index((row, slot)), rows, :]
        index, flip, source = FROM_QUARTER[(row, slot)]
        quarter = self.quarter_ref[index]
        far_rows = quarter.T if flip else quarter
        own_rows = self.mine(source[0], source[1], self.far).T
        return jnp.where(
            self.side == 0,
            jnp.concatenate([own_rows, far_rows], axis=0),
            jnp.concatenate([far_rows, own_rows], axis=0),
        )


def band_kernel(tiles, odd, parts, scaled, halo, quarters, side_ref, scale_ref, keep_ref, *rest):
    mine = Tiles(rest[:parts], scale_ref if scaled else None)
    other_refs = rest[parts : 2 * parts]
    rest = rest[2 * parts :]
    if halo is True:
        left_ref, right_ref = rest[:2]
        rest = rest[2:]
    if quarters:
        out_ref, quarter_ref, lh_ref, ll_ref, rh_ref, rl_ref = rest
    else:
        out_ref, lh_ref, ll_ref, rh_ref, rl_ref = rest
    tile = lh_ref.shape[1]
    half = tile // 2
    side = side_ref[0]
    own = pl.ds(pl.multiple_of(side * half, half), half)
    far = pl.ds(pl.multiple_of((1 - side) * half, half), half)
    if other_refs[0].shape[-2] == half:
        other = Rebuilt(other_refs[0], other_refs[1], mine, side, own, far)
    else:
        other = Tiles(other_refs, scale_ref if scaled else None)
    by_row = [[(index, slot) for index, (row, slot) in enumerate(tiles) if row == r] for r in range(2)]

    for row in range(2):
        for slot in range(5):
            high, low = split(jnp.concatenate([mine(row, slot), other(row, slot)], axis=1))
            lh_ref[row, :, slot * tile : (slot + 1) * tile] = high
            ll_ref[row, :, slot * tile : (slot + 1) * tile] = low
        for offset in range(5):
            k = row + offset - 2
            for place, (index, slot) in enumerate(by_row[row]):
                col = row + slot - 2
                where = (row, slice(offset * tile, (offset + 1) * tile), slice(place * half, (place + 1) * half))
                if abs(k - col) > 2 or (halo == "skip" and k not in (0, 1) and col not in (0, 1)):
                    rh_ref[where] = jnp.zeros((tile, half), jnp.bfloat16)
                    rl_ref[where] = jnp.zeros((tile, half), jnp.bfloat16)
                    continue
                if k in (0, 1):
                    b = col - k + 2
                    right = jnp.concatenate([mine(k, b, own), mine(k, b, far)], axis=0)
                elif col not in (0, 1):
                    src = left_ref if k < 0 else right_ref
                    b = 2 * (k + 2) + (col + 2) if k < 0 else 2 * (k - 2) + (col - 2)
                    right = jnp.concatenate([src[b, own, :], src[b, far, :]], axis=0)
                else:
                    s = k - col + 2
                    right = jnp.concatenate([mine(col, s, own), other(col, s, own)], axis=1).T
                high, low = split(right)
                rh_ref[where] = high
                rl_ref[where] = low
    for row in range(2):
        def one(x, y):
            return lax.dot_general(x, y, CONTRACT, preferred_element_type=jnp.float32)
        a_high = lh_ref[row]
        b_high = rh_ref[row]
        acc = one(ll_ref[row], b_high) + one(a_high, rl_ref[row]) + one(a_high, b_high)
        for place, (index, slot) in enumerate(by_row[row]):
            value = acc[:, place * half : (place + 1) * half]
            if halo == "skip":
                out_ref[row, slot] = value
                continue
            if odd:
                value = 2.0 * mine(row, slot) - value
            value = value * keep_ref[row, slot].astype(jnp.float32)
            if len(tiles) == len(ALL):
                out_ref[row, slot] = value
            else:
                out_ref[index] = value
    if quarters:
        for index, key in enumerate(QUARTERS):
            quarter_ref[index] = out_ref[tiles.index(key), own, :]


def band_call(tiles, odd, side, scale, keep, mine, other, halo=None, scaled=False, quarters=False):
    smem = pl.BlockSpec(memory_space=pltpu.SMEM)
    vmem = pl.BlockSpec(memory_space=pltpu.VMEM)
    args = [side, scale, keep] + list(mine) + list(other) + (list(halo) if isinstance(halo, tuple) else [])
    half = mine[0].shape[-1]
    tile = (mine[0].shape[-2], half)
    shape = (2, 5) + tile if len(tiles) == len(ALL) else (len(tiles),) + tile
    width = len(tiles) // 2
    lefts = (2, tile[0], 5 * 2 * half)
    rights = (2, 5 * tile[0], width * half)
    out_shape = jax.ShapeDtypeStruct(shape, jnp.float32)
    if quarters:
        out_shape = (out_shape, jax.ShapeDtypeStruct((len(QUARTERS), half, half), jnp.float32))
    return pl.pallas_call(
        functools.partial(band_kernel, tiles, odd, len(mine), scaled, halo if halo == "skip" else halo is not None, quarters),
        out_shape=out_shape,
        in_specs=[smem, smem, smem] + [vmem] * (len(args) - 3),
        out_specs=(vmem, vmem) if quarters else vmem,
        scratch_shapes=[pltpu.VMEM(lefts, jnp.bfloat16)] * 2 + [pltpu.VMEM(rights, jnp.bfloat16)] * 2,
    )(*args)


def finish_kernel(side_ref, keep_ref, partial_ref, diag_ref, off_ref, off_other_ref, left_ref, right_ref, out_ref):
    half = out_ref.shape[3]
    side = side_ref[0]
    own = pl.ds(pl.multiple_of(side * half, half), half)
    far = pl.ds(pl.multiple_of((1 - side) * half, half), half)
    for row in range(2):
        for slot in range(5):
            col = row + slot - 2
            value = partial_ref[row, slot]
            if (row, slot) in DIAG:
                mine = diag_ref[DIAG.index((row, slot))]
            else:
                mine = off_ref[OFF.index((row, slot))]
                for k in range(max(row, col) - 2, min(row, col) + 3):
                    if k in (0, 1):
                        continue
                    index = OFF.index((row, k - row + 2))
                    full = jnp.concatenate([off_ref[index], off_other_ref[index]], axis=1)
                    high, low = split(full)
                    src = left_ref if k < 0 else right_ref
                    b = 2 * (k + 2) + (col + 2) if k < 0 else 2 * (k - 2) + (col - 2)
                    right = jnp.concatenate([src[b, own, :], src[b, far, :]], axis=0)
                    value = value + dot3(high, low, right, CONTRACT)
            out_ref[row, slot] = (2.0 * mine - value) * keep_ref[row, slot].astype(jnp.float32)


def finish(side, keep, partial, diag, off, off_other, halo):
    smem = pl.BlockSpec(memory_space=pltpu.SMEM)
    vmem = pl.BlockSpec(memory_space=pltpu.VMEM)
    return pl.pallas_call(
        finish_kernel,
        out_shape=jax.ShapeDtypeStruct(partial.shape, jnp.float32),
        in_specs=[smem, smem] + [vmem] * 6,
        out_specs=vmem,
    )(side, keep, partial, diag, off, off_other, halo[0], halo[1])


def block_kernel(pattern_ref, density_ref, out_ref):
    for index, (row, slot) in enumerate(DIAG):
        out_ref[index] = density_ref[row, slot] * pattern_ref[row, slot].astype(jnp.float32)


def first_block(pattern, density):
    return pl.pallas_call(
        block_kernel,
        out_shape=jax.ShapeDtypeStruct((len(DIAG),) + density.shape[2:], jnp.float32),
        in_specs=[pl.BlockSpec(memory_space=pltpu.SMEM), pl.BlockSpec(memory_space=pltpu.VMEM)],
        out_specs=pl.BlockSpec(memory_space=pltpu.VMEM),
    )(pattern, density)


def purify(density, pattern, truncation):
    side = lax.axis_index("help").astype(jnp.int32).reshape(1)
    halo = send_block(first_block(pattern, density))
    other = swap_help(density)
    diag, quarter = band_call(DIAG, False, side, pattern, truncation[0], [density], [other], scaled=True, quarters=True)
    next_halo = send_block(diag)
    quarter_other = swap_help(quarter)
    off = band_call(OFF, False, side, pattern, truncation[0], [density], [other], halo, scaled=True)
    off_other = swap_help(off)
    partial = band_call(ALL, True, side, pattern, truncation[1], [diag, off], [quarter_other, off_other], "skip")
    return finish(side, truncation[1], partial, diag, off, off_other, next_halo)


def solution(mesh):
    return jax.shard_map(
        purify,
        mesh=mesh,
        in_specs=(P("rows", None, None, "help"), P("rows", None), P(None, "rows", None)),
        out_specs=P("rows", None, None, "help"),
        check_vma=False,
    )
```

```python
import functools

import jax
import jax.numpy as jnp
from jax import lax
from jax.experimental import pallas as pl
from jax.experimental.pallas import tpu as pltpu
from jax.sharding import PartitionSpec as P


DIAG = ((0, 2), (0, 3), (1, 1), (1, 2))
OFF = ((0, 0), (0, 1), (0, 4), (1, 0), (1, 3), (1, 4))
ALL = tuple((row, slot) for row in range(2) for slot in range(5))
CONTRACT = (((1,), (0,)), ((), ()))


def swap_help(value):
    return lax.ppermute(value, "help", [(0, 1), (1, 0)])


def send_block(block):
    count = lax.axis_size("rows")
    from_left = lax.ppermute(block, "rows", [(i, i + 1) for i in range(count - 1)])
    from_right = lax.ppermute(block, "rows", [(i + 1, i) for i in range(count - 1)])
    return from_left, from_right


def split(x):
    high = x.astype(jnp.bfloat16)
    return high, (x - high.astype(jnp.float32)).astype(jnp.bfloat16)


class Tiles:
    def __init__(self, refs, scale):
        self.refs = refs
        self.scale = scale

    def __call__(self, row, slot, rows=slice(None)):
        if len(self.refs) == 1:
            value = self.refs[0][row, slot, rows, :]
        elif (row, slot) in DIAG:
            value = self.refs[0][DIAG.index((row, slot)), rows, :]
        else:
            value = self.refs[1][OFF.index((row, slot)), rows, :]
        if self.scale is not None:
            value = value * self.scale[row, slot].astype(jnp.float32)
        return value


QUARTERS = ((0, 2), (0, 3), (1, 2))
FROM_QUARTER = {(0, 2): (0, False, (0, 2)), (0, 3): (1, False, (1, 1)), (1, 1): (1, True, (0, 3)), (1, 2): (2, False, (1, 2))}


class Rebuilt:
    def __init__(self, quarter_ref, off_ref, mine, side, own, far):
        self.quarter_ref, self.off_ref, self.mine = quarter_ref, off_ref, mine
        self.side, self.own, self.far = side, own, far

    def __call__(self, row, slot, rows=slice(None)):
        if (row, slot) not in DIAG:
            return self.off_ref[OFF.index((row, slot)), rows, :]
        index, flip, source = FROM_QUARTER[(row, slot)]
        quarter = self.quarter_ref[index]
        far_rows = quarter.T if flip else quarter
        own_rows = self.mine(source[0], source[1], self.far).T
        return jnp.where(
            self.side == 0,
            jnp.concatenate([own_rows, far_rows], axis=0),
            jnp.concatenate([far_rows, own_rows], axis=0),
        )


def band_kernel(tiles, odd, parts, scaled, mode, quarters, side_ref, scale_ref, keep_ref, *rest):
    mine = Tiles(rest[:parts], scale_ref if scaled else None)
    rest = rest[parts:]
    other_refs = rest[: len(rest) - 5 - (3 if mode == "halo" else (2 if mode == "plain" else 0)) - (1 if quarters else 0)]
    rest = rest[len(other_refs) :]
    if mode in ("plain", "halo"):
        left_ref, right_ref = rest[:2]
        rest = rest[2:]
    if mode == "halo":
        partial_ref = rest[0]
        rest = rest[1:]
    if quarters:
        out_ref, quarter_ref, lh_ref, ll_ref, rh_ref, rl_ref = rest
    else:
        out_ref, lh_ref, ll_ref, rh_ref, rl_ref = rest
    tile = lh_ref.shape[1]
    half = tile // 2
    side = side_ref[0]
    own = pl.ds(pl.multiple_of(side * half, half), half)
    far = pl.ds(pl.multiple_of((1 - side) * half, half), half)
    if other_refs[0].shape[-2] == half:
        other = Rebuilt(other_refs[0], other_refs[1] if len(other_refs) > 1 else None, mine, side, own, far)
    else:
        other = Tiles(other_refs, scale_ref if scaled else None)
    by_row = [[(index, slot) for index, (row, slot) in enumerate(tiles) if row == r] for r in range(2)]

    def wanted(k):
        if mode == "own":
            return k in (0, 1)
        if mode == "halo":
            return k not in (0, 1)
        return True

    for row in range(2):
        offsets = [o for o in range(5) if wanted(row + o - 2)]
        for place_k, offset in enumerate(offsets):
            high, low = split(jnp.concatenate([mine(row, offset), other(row, offset)], axis=1))
            lh_ref[row, :, place_k * tile : (place_k + 1) * tile] = high
            ll_ref[row, :, place_k * tile : (place_k + 1) * tile] = low
            k = row + offset - 2
            for place, (index, slot) in enumerate(by_row[row]):
                col = row + slot - 2
                where = (row, slice(place_k * tile, (place_k + 1) * tile), slice(place * half, (place + 1) * half))
                if abs(k - col) > 2:
                    rh_ref[where] = jnp.zeros((tile, half), jnp.bfloat16)
                    rl_ref[where] = jnp.zeros((tile, half), jnp.bfloat16)
                    continue
                if k in (0, 1):
                    b = col - k + 2
                    right = jnp.concatenate([mine(k, b, own), mine(k, b, far)], axis=0)
                elif col not in (0, 1):
                    src = left_ref if k < 0 else right_ref
                    b = 2 * (k + 2) + (col + 2) if k < 0 else 2 * (k - 2) + (col - 2)
                    right = jnp.concatenate([src[b, own, :], src[b, far, :]], axis=0)
                else:
                    s = k - col + 2
                    right = jnp.concatenate([mine(col, s, own), other(col, s, own)], axis=1).T
                high, low = split(right)
                rh_ref[where] = high
                rl_ref[where] = low
    for row in range(2):
        def one(x, y):
            return lax.dot_general(x, y, CONTRACT, preferred_element_type=jnp.float32)

        a_high = lh_ref[row]
        b_high = rh_ref[row]
        acc = one(ll_ref[row], b_high) + one(a_high, rl_ref[row]) + one(a_high, b_high)
        for place, (index, slot) in enumerate(by_row[row]):
            value = acc[:, place * half : (place + 1) * half]
            if mode == "own":
                out_ref[row, slot] = value
                continue
            if mode == "halo":
                value = value + partial_ref[row, slot]
            if odd:
                value = 2.0 * mine(row, slot) - value
            value = value * keep_ref[row, slot].astype(jnp.float32)
            if len(tiles) == len(ALL):
                out_ref[row, slot] = value
            else:
                out_ref[index] = value
    if quarters:
        for index, key in enumerate(QUARTERS):
            quarter_ref[index] = out_ref[tiles.index(key), own, :]


def band_call(tiles, odd, side, scale, keep, mine, other, halo=None, scaled=False, quarters=False, mode=None, partial=None):
    smem = pl.BlockSpec(memory_space=pltpu.SMEM)
    vmem = pl.BlockSpec(memory_space=pltpu.VMEM)
    if mode is None:
        mode = "plain" if halo is not None else "none"
    args = [side, scale, keep] + list(mine) + list(other)
    if halo is not None:
        args += list(halo)
    if partial is not None:
        args.append(partial)
    half = mine[0].shape[-1]
    tile = (mine[0].shape[-2], half)
    shape = (2, 5) + tile if len(tiles) == len(ALL) else (len(tiles),) + tile
    width = len(tiles) // 2
    count = {"own": 2, "halo": 3}.get(mode, 5)
    lefts = (2, tile[0], count * 2 * half)
    rights = (2, count * tile[0], width * half)
    out_shape = jax.ShapeDtypeStruct(shape, jnp.float32)
    if quarters:
        out_shape = (out_shape, jax.ShapeDtypeStruct((len(QUARTERS), half, half), jnp.float32))
    return pl.pallas_call(
        functools.partial(band_kernel, tiles, odd, len(mine), scaled, mode, quarters),
        out_shape=out_shape,
        in_specs=[smem, smem, smem] + [vmem] * (len(args) - 3),
        out_specs=(vmem, vmem) if quarters else vmem,
        scratch_shapes=[pltpu.VMEM(lefts, jnp.bfloat16)] * 2 + [pltpu.VMEM(rights, jnp.bfloat16)] * 2,
    )(*args)


def block_kernel(pattern_ref, density_ref, out_ref):
    for index, (row, slot) in enumerate(DIAG):
        out_ref[index] = density_ref[row, slot] * pattern_ref[row, slot].astype(jnp.float32)


def first_block(pattern, density):
    return pl.pallas_call(
        block_kernel,
        out_shape=jax.ShapeDtypeStruct((len(DIAG),) + density.shape[2:], jnp.float32),
        in_specs=[pl.BlockSpec(memory_space=pltpu.SMEM), pl.BlockSpec(memory_space=pltpu.VMEM)],
        out_specs=pl.BlockSpec(memory_space=pltpu.VMEM),
    )(pattern, density)


def purify(density, pattern, truncation):
    side = lax.axis_index("help").astype(jnp.int32).reshape(1)
    halo = send_block(first_block(pattern, density))
    other = swap_help(density)
    diag, quarter = band_call(DIAG, False, side, pattern, truncation[0], [density], [other], scaled=True, quarters=True)
    next_halo = send_block(diag)
    quarter_other = swap_help(quarter)
    off = band_call(OFF, False, side, pattern, truncation[0], [density], [other], halo, scaled=True)
    off_other = swap_help(off)
    partial = band_call(ALL, True, side, pattern, truncation[1], [diag, off], [quarter_other], mode="own")
    return band_call(
        ALL, True, side, pattern, truncation[1], [diag, off], [quarter_other, off_other], next_halo, mode="halo", partial=partial
    )


def solution(mesh):
    return jax.shard_map(
        purify,
        mesh=mesh,
        in_specs=(P("rows", None, None, "help"), P("rows", None), P(None, "rows", None)),
        out_specs=P("rows", None, None, "help"),
        check_vma=False,
    )
```

```python
import functools

import jax
import jax.numpy as jnp
from jax import lax
from jax.experimental import pallas as pl
from jax.experimental.pallas import tpu as pltpu
from jax.sharding import PartitionSpec as P


DIAG = ((0, 2), (0, 3), (1, 1), (1, 2))
OFF = ((0, 0), (0, 1), (0, 4), (1, 0), (1, 3), (1, 4))
ALL = tuple((row, slot) for row in range(2) for slot in range(5))
CONTRACT = (((1,), (0,)), ((), ()))
PRECISION = lax.Precision.HIGH


def swap_help(value):
    return lax.ppermute(value, "help", [(0, 1), (1, 0)])


def send_block(block):
    count = lax.axis_size("rows")
    from_left = lax.ppermute(block, "rows", [(i, i + 1) for i in range(count - 1)])
    from_right = lax.ppermute(block, "rows", [(i + 1, i) for i in range(count - 1)])
    return from_left, from_right


class Tiles:
    def __init__(self, refs, scale):
        self.refs = refs
        self.scale = scale

    def __call__(self, row, slot, rows=slice(None)):
        if len(self.refs) == 1:
            value = self.refs[0][row, slot, rows, :]
        elif (row, slot) in DIAG:
            value = self.refs[0][DIAG.index((row, slot)), rows, :]
        else:
            value = self.refs[1][OFF.index((row, slot)), rows, :]
        if self.scale is not None:
            value = value * self.scale[row, slot].astype(jnp.float32)
        return value


QUARTERS = ((0, 2), (0, 3), (1, 2))
FROM_QUARTER = {(0, 2): (0, False, (0, 2)), (0, 3): (1, False, (1, 1)), (1, 1): (1, True, (0, 3)), (1, 2): (2, False, (1, 2))}


class Rebuilt:
    def __init__(self, quarter_ref, off_ref, mine, side, own, far):
        self.quarter_ref, self.off_ref, self.mine = quarter_ref, off_ref, mine
        self.side, self.own, self.far = side, own, far

    def __call__(self, row, slot, rows=slice(None)):
        if (row, slot) not in DIAG:
            return self.off_ref[OFF.index((row, slot)), rows, :]
        index, flip, source = FROM_QUARTER[(row, slot)]
        quarter = self.quarter_ref[index]
        far_rows = quarter.T if flip else quarter
        own_rows = self.mine(source[0], source[1], self.far).T
        return jnp.where(
            self.side == 0,
            jnp.concatenate([own_rows, far_rows], axis=0),
            jnp.concatenate([far_rows, own_rows], axis=0),
        )


def band_kernel(tiles, odd, parts, scaled, mode, quarters, side_ref, scale_ref, keep_ref, *rest):
    mine = Tiles(rest[:parts], scale_ref if scaled else None)
    rest = rest[parts:]
    other_refs = rest[: len(rest) - 3 - (3 if mode == "halo" else (2 if mode == "plain" else 0)) - (1 if quarters else 0)]
    rest = rest[len(other_refs) :]
    if mode in ("plain", "halo"):
        left_ref, right_ref = rest[:2]
        rest = rest[2:]
    if mode == "halo":
        partial_ref = rest[0]
        rest = rest[1:]
    if quarters:
        out_ref, quarter_ref, lh_ref, rh_ref = rest
    else:
        out_ref, lh_ref, rh_ref = rest
    tile = lh_ref.shape[1]
    half = tile // 2
    side = side_ref[0]
    own = pl.ds(pl.multiple_of(side * half, half), half)
    far = pl.ds(pl.multiple_of((1 - side) * half, half), half)
    if other_refs[0].shape[-2] == half:
        other = Rebuilt(other_refs[0], other_refs[1] if len(other_refs) > 1 else None, mine, side, own, far)
    else:
        other = Tiles(other_refs, scale_ref if scaled else None)
    by_row = [[(index, slot) for index, (row, slot) in enumerate(tiles) if row == r] for r in range(2)]

    def wanted(k):
        if mode == "own":
            return k in (0, 1)
        if mode == "halo":
            return k not in (0, 1)
        return True

    for row in range(2):
        offsets = [o for o in range(5) if wanted(row + o - 2)]
        for place_k, offset in enumerate(offsets):
            lh_ref[row, :, place_k * tile : (place_k + 1) * tile] = jnp.concatenate([mine(row, offset), other(row, offset)], axis=1)
            k = row + offset - 2
            for place, (index, slot) in enumerate(by_row[row]):
                col = row + slot - 2
                where = (row, slice(place_k * tile, (place_k + 1) * tile), slice(place * half, (place + 1) * half))
                if abs(k - col) > 2:
                    rh_ref[where] = jnp.zeros((tile, half), jnp.float32)
                    continue
                if k in (0, 1):
                    b = col - k + 2
                    right = jnp.concatenate([mine(k, b, own), mine(k, b, far)], axis=0)
                elif col not in (0, 1):
                    src = left_ref if k < 0 else right_ref
                    b = 2 * (k + 2) + (col + 2) if k < 0 else 2 * (k - 2) + (col - 2)
                    right = jnp.concatenate([src[b, own, :], src[b, far, :]], axis=0)
                else:
                    s = k - col + 2
                    right = jnp.concatenate([mine(col, s, own), other(col, s, own)], axis=1).T
                rh_ref[where] = right
    for row in range(2):
        acc = lax.dot_general(lh_ref[row], rh_ref[row], CONTRACT, precision=PRECISION, preferred_element_type=jnp.float32)
        for place, (index, slot) in enumerate(by_row[row]):
            value = acc[:, place * half : (place + 1) * half]
            if mode == "own":
                out_ref[row, slot] = value
                continue
            if mode == "halo":
                value = value + partial_ref[row, slot]
            if odd:
                value = 2.0 * mine(row, slot) - value
            value = value * keep_ref[row, slot].astype(jnp.float32)
            if len(tiles) == len(ALL):
                out_ref[row, slot] = value
            else:
                out_ref[index] = value
    if quarters:
        for index, key in enumerate(QUARTERS):
            quarter_ref[index] = out_ref[tiles.index(key), own, :]


def band_call(tiles, odd, side, scale, keep, mine, other, halo=None, scaled=False, quarters=False, mode=None, partial=None):
    smem = pl.BlockSpec(memory_space=pltpu.SMEM)
    vmem = pl.BlockSpec(memory_space=pltpu.VMEM)
    if mode is None:
        mode = "plain" if halo is not None else "none"
    args = [side, scale, keep] + list(mine) + list(other)
    if halo is not None:
        args += list(halo)
    if partial is not None:
        args.append(partial)
    half = mine[0].shape[-1]
    tile = (mine[0].shape[-2], half)
    shape = (2, 5) + tile if len(tiles) == len(ALL) else (len(tiles),) + tile
    width = len(tiles) // 2
    count = {"own": 2, "halo": 3}.get(mode, 5)
    lefts = (2, tile[0], count * 2 * half)
    rights = (2, count * tile[0], width * half)
    out_shape = jax.ShapeDtypeStruct(shape, jnp.float32)
    if quarters:
        out_shape = (out_shape, jax.ShapeDtypeStruct((len(QUARTERS), half, half), jnp.float32))
    return pl.pallas_call(
        functools.partial(band_kernel, tiles, odd, len(mine), scaled, mode, quarters),
        out_shape=out_shape,
        in_specs=[smem, smem, smem] + [vmem] * (len(args) - 3),
        out_specs=(vmem, vmem) if quarters else vmem,
        scratch_shapes=[pltpu.VMEM(lefts, jnp.float32), pltpu.VMEM(rights, jnp.float32)],
    )(*args)


def block_kernel(pattern_ref, density_ref, out_ref):
    for index, (row, slot) in enumerate(DIAG):
        out_ref[index] = density_ref[row, slot] * pattern_ref[row, slot].astype(jnp.float32)


def first_block(pattern, density):
    return pl.pallas_call(
        block_kernel,
        out_shape=jax.ShapeDtypeStruct((len(DIAG),) + density.shape[2:], jnp.float32),
        in_specs=[pl.BlockSpec(memory_space=pltpu.SMEM), pl.BlockSpec(memory_space=pltpu.VMEM)],
        out_specs=pl.BlockSpec(memory_space=pltpu.VMEM),
    )(pattern, density)


def purify(density, pattern, truncation):
    side = lax.axis_index("help").astype(jnp.int32).reshape(1)
    halo = send_block(first_block(pattern, density))
    other = swap_help(density)
    diag, quarter = band_call(DIAG, False, side, pattern, truncation[0], [density], [other], scaled=True, quarters=True)
    next_halo = send_block(diag)
    quarter_other = swap_help(quarter)
    off = band_call(OFF, False, side, pattern, truncation[0], [density], [other], halo, scaled=True)
    off_other = swap_help(off)
    partial = band_call(ALL, True, side, pattern, truncation[1], [diag, off], [quarter_other], mode="own")
    return band_call(
        ALL, True, side, pattern, truncation[1], [diag, off], [quarter_other, off_other], next_halo, mode="halo", partial=partial
    )


def solution(mesh):
    return jax.shard_map(
        purify,
        mesh=mesh,
        in_specs=(P("rows", None, None, "help"), P("rows", None), P(None, "rows", None)),
        out_specs=P("rows", None, None, "help"),
        check_vma=False,
    )
```

```python
import functools

import jax
import jax.numpy as jnp
from jax import lax
from jax.experimental import pallas as pl
from jax.experimental.pallas import tpu as pltpu
from jax.sharding import PartitionSpec as P


DIAG = ((0, 2), (0, 3), (1, 1), (1, 2))
OFF = ((0, 0), (0, 1), (0, 4), (1, 0), (1, 3), (1, 4))
ALL = tuple((row, slot) for row in range(2) for slot in range(5))
CONTRACT = (((1,), (0,)), ((), ()))


def swap_help(value):
    return lax.ppermute(value, "help", [(0, 1), (1, 0)])


def send_block(block):
    count = lax.axis_size("rows")
    from_left = lax.ppermute(block, "rows", [(i, i + 1) for i in range(count - 1)])
    from_right = lax.ppermute(block, "rows", [(i + 1, i) for i in range(count - 1)])
    return from_left, from_right


def split(x):
    high = x.astype(jnp.bfloat16)
    return high, (x - high.astype(jnp.float32)).astype(jnp.bfloat16)


class Tiles:
    def __init__(self, refs, scale):
        self.refs = refs
        self.scale = scale

    def __call__(self, row, slot, rows=slice(None)):
        if len(self.refs) == 1:
            value = self.refs[0][row, slot, rows, :]
        elif (row, slot) in DIAG:
            value = self.refs[0][DIAG.index((row, slot)), rows, :]
        else:
            value = self.refs[1][OFF.index((row, slot)), rows, :]
        if self.scale is not None:
            value = value * self.scale[row, slot].astype(jnp.float32)
        return value


QUARTERS = ((0, 2), (0, 3), (1, 2))
FROM_QUARTER = {(0, 2): (0, False, (0, 2)), (0, 3): (1, False, (1, 1)), (1, 1): (1, True, (0, 3)), (1, 2): (2, False, (1, 2))}


class Rebuilt:
    def __init__(self, quarter_ref, off_ref, mine, side, own, far):
        self.quarter_ref, self.off_ref, self.mine = quarter_ref, off_ref, mine
        self.side, self.own, self.far = side, own, far

    def __call__(self, row, slot, rows=slice(None)):
        if (row, slot) not in DIAG:
            return self.off_ref[OFF.index((row, slot)), rows, :]
        index, flip, source = FROM_QUARTER[(row, slot)]
        quarter = self.quarter_ref[index]
        far_rows = quarter.T if flip else quarter
        own_rows = self.mine(source[0], source[1], self.far).T
        return jnp.where(
            self.side == 0,
            jnp.concatenate([own_rows, far_rows], axis=0),
            jnp.concatenate([far_rows, own_rows], axis=0),
        )


def band_kernel(tiles, odd, parts, scaled, mode, quarters, side_ref, scale_ref, keep_ref, *rest):
    mine = Tiles(rest[:parts], scale_ref if scaled else None)
    rest = rest[parts:]
    extra = {"halo": 3, "plain": 2, "scaled": 4}.get(mode, 0)
    other_refs = rest[: len(rest) - 5 - extra - (1 if quarters else 0)]
    rest = rest[len(other_refs) :]
    neighbour_scale = None
    if mode in ("plain", "halo", "scaled"):
        left_ref, right_ref = rest[:2]
        rest = rest[2:]
    if mode == "scaled":
        neighbour_scale = rest[:2]
        rest = rest[2:]
    if mode == "halo":
        partial_ref = rest[0]
        rest = rest[1:]
    if quarters:
        out_ref, quarter_ref, lh_ref, ll_ref, rh_ref, rl_ref = rest
    else:
        out_ref, lh_ref, ll_ref, rh_ref, rl_ref = rest
    tile = lh_ref.shape[1]
    half = tile // 2
    side = side_ref[0]
    own = pl.ds(pl.multiple_of(side * half, half), half)
    far = pl.ds(pl.multiple_of((1 - side) * half, half), half)
    if other_refs[0].shape[-2] == half:
        other = Rebuilt(other_refs[0], other_refs[1] if len(other_refs) > 1 else None, mine, side, own, far)
    else:
        other = Tiles(other_refs, scale_ref if scaled else None)
    by_row = [[(index, slot) for index, (row, slot) in enumerate(tiles) if row == r] for r in range(2)]

    def wanted(k):
        if mode == "own":
            return k in (0, 1)
        if mode == "halo":
            return k not in (0, 1)
        return True

    for row in range(2):
        offsets = [o for o in range(5) if wanted(row + o - 2)]
        for place_k, offset in enumerate(offsets):
            high, low = split(jnp.concatenate([mine(row, offset), other(row, offset)], axis=1))
            lh_ref[row, :, place_k * tile : (place_k + 1) * tile] = high
            ll_ref[row, :, place_k * tile : (place_k + 1) * tile] = low
            k = row + offset - 2
            for place, (index, slot) in enumerate(by_row[row]):
                col = row + slot - 2
                where = (row, slice(place_k * tile, (place_k + 1) * tile), slice(place * half, (place + 1) * half))
                if abs(k - col) > 2:
                    rh_ref[where] = jnp.zeros((tile, half), jnp.bfloat16)
                    rl_ref[where] = jnp.zeros((tile, half), jnp.bfloat16)
                    continue
                if k in (0, 1):
                    b = col - k + 2
                    right = jnp.concatenate([mine(k, b, own), mine(k, b, far)], axis=0)
                elif col not in (0, 1):
                    src = left_ref if k < 0 else right_ref
                    b = 2 * (k + 2) + (col + 2) if k < 0 else 2 * (k - 2) + (col - 2)
                    right = jnp.concatenate([src[b, own, :], src[b, far, :]], axis=0)
                    if neighbour_scale is not None:
                        row_n, slot_n = DIAG[b]
                        factor = neighbour_scale[0 if k < 0 else 1][row_n, slot_n]
                        right = right * factor.astype(jnp.float32)
                else:
                    s = k - col + 2
                    right = jnp.concatenate([mine(col, s, own), other(col, s, own)], axis=1).T
                high, low = split(right)
                rh_ref[where] = high
                rl_ref[where] = low

    def one(x, y):
        return lax.dot_general(x, y, CONTRACT, preferred_element_type=jnp.float32)

    for row in range(2):
        offsets = [o for o in range(5) if wanted(row + o - 2)]
        row_tiles = by_row[row]
        values = []
        for first in range(0, len(row_tiles), 2):
            chunk = range(first, min(first + 2, len(row_tiles)))
            used = [
                place_k
                for place_k, offset in enumerate(offsets)
                if any(abs(offset - row_tiles[place][1]) <= 2 for place in chunk)
            ]
            ks = slice(used[0] * tile, (used[-1] + 1) * tile)
            ns = slice(chunk[0] * half, (chunk[-1] + 1) * half)
            a_high = lh_ref[row, :, ks]
            b_high = rh_ref[row, ks, ns]
            acc = one(ll_ref[row, :, ks], b_high) + one(a_high, rl_ref[row, ks, ns]) + one(a_high, b_high)
            values += [acc[:, n * half : (n + 1) * half] for n in range(len(chunk))]
        for place, (index, slot) in enumerate(row_tiles):
            value = values[place]
            if mode == "own":
                out_ref[row, slot] = value
                continue
            if mode == "halo":
                value = value + partial_ref[row, slot]
            if odd:
                value = 2.0 * mine(row, slot) - value
            value = value * keep_ref[row, slot].astype(jnp.float32)
            if len(tiles) == len(ALL):
                out_ref[row, slot] = value
            else:
                out_ref[index] = value
    if quarters:
        for index, key in enumerate(QUARTERS):
            quarter_ref[index] = out_ref[tiles.index(key), own, :]


def band_call(
    tiles, odd, side, scale, keep, mine, other, halo=None, scaled=False, quarters=False, mode=None, partial=None, halo_scale=None
):
    smem = pl.BlockSpec(memory_space=pltpu.SMEM)
    vmem = pl.BlockSpec(memory_space=pltpu.VMEM)
    if mode is None:
        mode = "plain" if halo is not None else "none"
    if halo_scale is not None:
        mode = "scaled"
    args = [side, scale, keep] + list(mine) + list(other)
    if halo is not None:
        args += list(halo)
    if partial is not None:
        args.append(partial)
    half = mine[0].shape[-1]
    tile = (mine[0].shape[-2], half)
    shape = (2, 5) + tile if len(tiles) == len(ALL) else (len(tiles),) + tile
    width = len(tiles) // 2
    count = {"own": 2, "halo": 3}.get(mode, 5)
    lefts = (2, tile[0], count * 2 * half)
    rights = (2, count * tile[0], width * half)
    out_shape = jax.ShapeDtypeStruct(shape, jnp.float32)
    if quarters:
        out_shape = (out_shape, jax.ShapeDtypeStruct((len(QUARTERS), half, half), jnp.float32))
    return pl.pallas_call(
        functools.partial(band_kernel, tiles, odd, len(mine), scaled, mode, quarters),
        out_shape=out_shape,
        in_specs=[smem, smem, smem] + [vmem] * (len(args) - 3) + ([smem, smem] if halo_scale is not None else []),
        out_specs=(vmem, vmem) if quarters else vmem,
        scratch_shapes=[pltpu.VMEM(lefts, jnp.bfloat16)] * 2 + [pltpu.VMEM(rights, jnp.bfloat16)] * 2,
    )(*(args + ([] if halo_scale is None else list(halo_scale))))


def purify(density, pattern, truncation):
    side = lax.axis_index("help").astype(jnp.int32).reshape(1)
    halo = send_block(jnp.stack([density[row, slot] for row, slot in DIAG]))
    halo_scale = send_block(pattern)
    other = swap_help(density)
    diag, quarter = band_call(DIAG, False, side, pattern, truncation[0], [density], [other], scaled=True, quarters=True)
    next_halo = send_block(diag)
    quarter_other = swap_help(quarter)
    off = band_call(OFF, False, side, pattern, truncation[0], [density], [other], halo, scaled=True, halo_scale=halo_scale)
    off_other = swap_help(off)
    partial = band_call(ALL, True, side, pattern, truncation[1], [diag, off], [quarter_other], mode="own")
    return band_call(
        ALL, True, side, pattern, truncation[1], [diag, off], [quarter_other, off_other], next_halo, mode="halo", partial=partial
    )


def solution(mesh):
    return jax.shard_map(
        purify,
        mesh=mesh,
        in_specs=(P("rows", None, None, "help"), P("rows", None), P(None, "rows", None)),
        out_specs=P("rows", None, None, "help"),
        check_vma=False,
    )
```

```python
import functools

import jax
import jax.numpy as jnp
from jax import lax
from jax.experimental import pallas as pl
from jax.experimental.pallas import tpu as pltpu
from jax.sharding import PartitionSpec as P


DIAG = ((0, 2), (0, 3), (1, 1), (1, 2))
OFF = ((0, 0), (0, 1), (0, 4), (1, 0), (1, 3), (1, 4))
ALL = tuple((row, slot) for row in range(2) for slot in range(5))
CONTRACT = (((1,), (0,)), ((), ()))


def swap_help(value):
    return lax.ppermute(value, "help", [(0, 1), (1, 0)])


def send_block(block):
    count = lax.axis_size("rows")
    from_left = lax.ppermute(block, "rows", [(i, i + 1) for i in range(count - 1)])
    from_right = lax.ppermute(block, "rows", [(i + 1, i) for i in range(count - 1)])
    return from_left, from_right


def split(x):
    high = x.astype(jnp.bfloat16)
    return high, (x - high.astype(jnp.float32)).astype(jnp.bfloat16)


class Tiles:
    def __init__(self, refs, scale):
        self.refs = refs
        self.scale = scale

    def __call__(self, row, slot, rows=slice(None)):
        if len(self.refs) == 1:
            value = self.refs[0][row, slot, rows, :]
        elif (row, slot) in DIAG:
            value = self.refs[0][DIAG.index((row, slot)), rows, :]
        else:
            value = self.refs[1][OFF.index((row, slot)), rows, :]
        if self.scale is not None:
            value = value * self.scale[row, slot].astype(jnp.float32)
        return value


QUARTERS = ((0, 2), (0, 3), (1, 2))
FROM_QUARTER = {(0, 2): (0, False, (0, 2)), (0, 3): (1, False, (1, 1)), (1, 1): (1, True, (0, 3)), (1, 2): (2, False, (1, 2))}


class Rebuilt:
    def __init__(self, quarter_ref, off_ref, mine, side, own, far):
        self.quarter_ref, self.off_ref, self.mine = quarter_ref, off_ref, mine
        self.side, self.own, self.far = side, own, far

    def __call__(self, row, slot, rows=slice(None)):
        if (row, slot) not in DIAG:
            return self.off_ref[OFF.index((row, slot)), rows, :]
        index, flip, source = FROM_QUARTER[(row, slot)]
        quarter = self.quarter_ref[index]
        far_rows = quarter.T if flip else quarter
        own_rows = self.mine(source[0], source[1], self.far).T
        return jnp.where(
            self.side == 0,
            jnp.concatenate([own_rows, far_rows], axis=0),
            jnp.concatenate([far_rows, own_rows], axis=0),
        )


def band_kernel(tiles, odd, parts, scaled, mode, quarters, side_ref, scale_ref, keep_ref, *rest):
    mine = Tiles(rest[:parts], scale_ref if scaled else None)
    rest = rest[parts:]
    other_refs = rest[: len(rest) - 5 - (3 if mode == "halo" else (2 if mode == "plain" else 0)) - (1 if quarters else 0)]
    rest = rest[len(other_refs) :]
    if mode in ("plain", "halo"):
        left_ref, right_ref = rest[:2]
        rest = rest[2:]
    if mode == "halo":
        partial_ref = rest[0]
        rest = rest[1:]
    if quarters:
        out_ref, quarter_ref, lh_ref, ll_ref, rh_ref, rl_ref = rest
    else:
        out_ref, lh_ref, ll_ref, rh_ref, rl_ref = rest
    tile = lh_ref.shape[1]
    half = tile // 2
    side = side_ref[0]
    own = pl.ds(pl.multiple_of(side * half, half), half)
    far = pl.ds(pl.multiple_of((1 - side) * half, half), half)
    if other_refs[0].shape[-2] == half:
        other = Rebuilt(other_refs[0], other_refs[1] if len(other_refs) > 1 else None, mine, side, own, far)
    else:
        other = Tiles(other_refs, scale_ref if scaled else None)
    by_row = [[(index, slot) for index, (row, slot) in enumerate(tiles) if row == r] for r in range(2)]

    def wanted(k):
        if mode == "own":
            return k in (0, 1)
        if mode == "halo":
            return k not in (0, 1)
        return True

    for row in range(2):
        offsets = [o for o in range(5) if wanted(row + o - 2)]
        for place_k, offset in enumerate(offsets):
            high, low = split(jnp.concatenate([mine(row, offset), other(row, offset)], axis=1))
            lh_ref[row, :, place_k * tile : (place_k + 1) * tile] = high
            ll_ref[row, :, place_k * tile : (place_k + 1) * tile] = low
            k = row + offset - 2
            for place, (index, slot) in enumerate(by_row[row]):
                col = row + slot - 2
                where = (row, slice(place_k * tile, (place_k + 1) * tile), slice(place * half, (place + 1) * half))
                if abs(k - col) > 2:
                    rh_ref[where] = jnp.zeros((tile, half), jnp.bfloat16)
                    rl_ref[where] = jnp.zeros((tile, half), jnp.bfloat16)
                    continue
                if k in (0, 1):
                    b = col - k + 2
                    right = jnp.concatenate([mine(k, b, own), mine(k, b, far)], axis=0)
                elif col not in (0, 1):
                    src = left_ref if k < 0 else right_ref
                    b = 2 * (k + 2) + (col + 2) if k < 0 else 2 * (k - 2) + (col - 2)
                    right = jnp.concatenate([src[b, own, :], src[b, far, :]], axis=0)
                else:
                    s = k - col + 2
                    right = jnp.concatenate([mine(col, s, own), other(col, s, own)], axis=1).T
                high, low = split(right)
                rh_ref[where] = high
                rl_ref[where] = low

    def one(x, y):
        return lax.dot_general(x, y, CONTRACT, preferred_element_type=jnp.float32)

    for row in range(2):
        offsets = [o for o in range(5) if wanted(row + o - 2)]
        row_tiles = by_row[row]
        values = []
        for first in range(0, len(row_tiles), 2):
            chunk = range(first, min(first + 2, len(row_tiles)))
            used = [
                place_k
                for place_k, offset in enumerate(offsets)
                if any(abs(offset - row_tiles[place][1]) <= 2 for place in chunk)
            ]
            ks = slice(used[0] * tile, (used[-1] + 1) * tile)
            ns = slice(chunk[0] * half, (chunk[-1] + 1) * half)
            a_high = lh_ref[row, :, ks]
            b_high = rh_ref[row, ks, ns]
            acc = one(ll_ref[row, :, ks], b_high) + one(a_high, rl_ref[row, ks, ns]) + one(a_high, b_high)
            values += [acc[:, n * half : (n + 1) * half] for n in range(len(chunk))]
        for place, (index, slot) in enumerate(row_tiles):
            value = values[place]
            if mode == "own":
                out_ref[row, slot] = value
                continue
            if mode == "halo":
                value = value + partial_ref[row, slot]
            if odd:
                value = 2.0 * mine(row, slot) - value
            value = value * keep_ref[row, slot].astype(jnp.float32)
            if len(tiles) == len(ALL):
                out_ref[row, slot] = value
            else:
                out_ref[index] = value
    if quarters:
        for index, key in enumerate(QUARTERS):
            quarter_ref[index] = out_ref[tiles.index(key), own, :]


def band_call(tiles, odd, side, scale, keep, mine, other, halo=None, scaled=False, quarters=False, mode=None, partial=None):
    smem = pl.BlockSpec(memory_space=pltpu.SMEM)
    vmem = pl.BlockSpec(memory_space=pltpu.VMEM)
    if mode is None:
        mode = "plain" if halo is not None else "none"
    args = [side, scale, keep] + list(mine) + list(other)
    if halo is not None:
        args += list(halo)
    if partial is not None:
        args.append(partial)
    half = mine[0].shape[-1]
    tile = (mine[0].shape[-2], half)
    shape = (2, 5) + tile if len(tiles) == len(ALL) else (len(tiles),) + tile
    width = len(tiles) // 2
    count = {"own": 2, "halo": 3}.get(mode, 5)
    lefts = (2, tile[0], count * 2 * half)
    rights = (2, count * tile[0], width * half)
    out_shape = jax.ShapeDtypeStruct(shape, jnp.float32)
    if quarters:
        out_shape = (out_shape, jax.ShapeDtypeStruct((len(QUARTERS), half, half), jnp.float32))
    return pl.pallas_call(
        functools.partial(band_kernel, tiles, odd, len(mine), scaled, mode, quarters),
        out_shape=out_shape,
        in_specs=[smem, smem, smem] + [vmem] * (len(args) - 3),
        out_specs=(vmem, vmem) if quarters else vmem,
        scratch_shapes=[pltpu.VMEM(lefts, jnp.bfloat16)] * 2 + [pltpu.VMEM(rights, jnp.bfloat16)] * 2,
    )(*args)


def block_kernel(pattern_ref, density_ref, out_ref):
    for index, (row, slot) in enumerate(DIAG):
        out_ref[index] = density_ref[row, slot] * pattern_ref[row, slot].astype(jnp.float32)


def first_block(pattern, density):
    return pl.pallas_call(
        block_kernel,
        out_shape=jax.ShapeDtypeStruct((len(DIAG),) + density.shape[2:], jnp.float32),
        in_specs=[pl.BlockSpec(memory_space=pltpu.SMEM), pl.BlockSpec(memory_space=pltpu.VMEM)],
        out_specs=pl.BlockSpec(memory_space=pltpu.VMEM),
    )(pattern, density)


def purify(density, pattern, truncation):
    side = lax.axis_index("help").astype(jnp.int32).reshape(1)
    halo = send_block(first_block(pattern, density))
    other = swap_help(density)
    diag, quarter = band_call(DIAG, False, side, pattern, truncation[0], [density], [other], scaled=True, quarters=True)
    next_halo = send_block(diag)
    quarter_other = swap_help(quarter)
    off = band_call(OFF, False, side, pattern, truncation[0], [density], [other], halo, scaled=True)
    off_other = swap_help(off)
    partial = band_call(ALL, True, side, pattern, truncation[1], [diag, off], [quarter_other], mode="own")
    return band_call(
        ALL, True, side, pattern, truncation[1], [diag, off], [quarter_other, off_other], next_halo, mode="halo", partial=partial
    )


def solution(mesh):
    return jax.shard_map(
        purify,
        mesh=mesh,
        in_specs=(P("rows", None, None, "help"), P("rows", None), P(None, "rows", None)),
        out_specs=P("rows", None, None, "help"),
        check_vma=False,
    )
```

```python
import functools

import jax
import jax.numpy as jnp
from jax import lax
from jax.experimental import pallas as pl
from jax.experimental.pallas import tpu as pltpu
from jax.sharding import PartitionSpec as P


DIAG = ((0, 2), (0, 3), (1, 1), (1, 2))
OFF = ((0, 0), (0, 1), (0, 4), (1, 0), (1, 3), (1, 4))
ALL = tuple((row, slot) for row in range(2) for slot in range(5))
CONTRACT = (((1,), (0,)), ((), ()))


def swap_help(value):
    return lax.ppermute(value, "help", [(0, 1), (1, 0)])


def send_block(block):
    count = lax.axis_size("rows")
    from_left = lax.ppermute(block, "rows", [(i, i + 1) for i in range(count - 1)])
    from_right = lax.ppermute(block, "rows", [(i + 1, i) for i in range(count - 1)])
    return from_left, from_right


class Tiles:
    def __init__(self, refs, scale):
        self.refs = refs
        self.scale = scale

    def __call__(self, row, slot, rows=slice(None)):
        if len(self.refs) == 1:
            value = self.refs[0][row, slot, rows, :]
        elif (row, slot) in DIAG:
            value = self.refs[0][DIAG.index((row, slot)), rows, :]
        else:
            value = self.refs[1][OFF.index((row, slot)), rows, :]
        if self.scale is not None:
            value = value * self.scale[row, slot].astype(jnp.float32)
        return value


QUARTERS = ((0, 2), (0, 3), (1, 2))
FROM_QUARTER = {(0, 2): (0, False, (0, 2)), (0, 3): (1, False, (1, 1)), (1, 1): (1, True, (0, 3)), (1, 2): (2, False, (1, 2))}


class Rebuilt:
    def __init__(self, quarter_ref, off_ref, mine, side, own, far):
        self.quarter_ref, self.off_ref, self.mine = quarter_ref, off_ref, mine
        self.side, self.own, self.far = side, own, far

    def __call__(self, row, slot, rows=slice(None)):
        if (row, slot) not in DIAG:
            return self.off_ref[OFF.index((row, slot)), rows, :]
        index, flip, source = FROM_QUARTER[(row, slot)]
        quarter = self.quarter_ref[index]
        far_rows = quarter.T if flip else quarter
        own_rows = self.mine(source[0], source[1], self.far).T
        return jnp.where(
            self.side == 0,
            jnp.concatenate([own_rows, far_rows], axis=0),
            jnp.concatenate([far_rows, own_rows], axis=0),
        )


def band_kernel(tiles, odd, parts, scaled, mode, quarters, side_ref, scale_ref, keep_ref, *rest):
    mine = Tiles(rest[:parts], scale_ref if scaled else None)
    rest = rest[parts:]
    other_refs = rest[: len(rest) - 3 - (3 if mode == "halo" else (2 if mode == "plain" else 0)) - (1 if quarters else 0)]
    rest = rest[len(other_refs) :]
    if mode in ("plain", "halo"):
        left_ref, right_ref = rest[:2]
        rest = rest[2:]
    if mode == "halo":
        partial_ref = rest[0]
        rest = rest[1:]
    if quarters:
        out_ref, quarter_ref, lh_ref, rh_ref = rest
    else:
        out_ref, lh_ref, rh_ref = rest
    tile = lh_ref.shape[1]
    half = tile // 2
    side = side_ref[0]
    own = pl.ds(pl.multiple_of(side * half, half), half)
    far = pl.ds(pl.multiple_of((1 - side) * half, half), half)
    if other_refs[0].shape[-2] == half:
        other = Rebuilt(other_refs[0], other_refs[1] if len(other_refs) > 1 else None, mine, side, own, far)
    else:
        other = Tiles(other_refs, scale_ref if scaled else None)
    by_row = [[(index, slot) for index, (row, slot) in enumerate(tiles) if row == r] for r in range(2)]

    def wanted(k):
        if mode == "own":
            return k in (0, 1)
        if mode == "halo":
            return k not in (0, 1)
        return True

    for row in range(2):
        offsets = [o for o in range(5) if wanted(row + o - 2)]
        for place_k, offset in enumerate(offsets):
            lh_ref[row, :, place_k * tile : (place_k + 1) * tile] = jnp.concatenate([mine(row, offset), other(row, offset)], axis=1)
            k = row + offset - 2
            for place, (index, slot) in enumerate(by_row[row]):
                col = row + slot - 2
                where = (row, slice(place_k * tile, (place_k + 1) * tile), slice(place * half, (place + 1) * half))
                if abs(k - col) > 2:
                    rh_ref[where] = jnp.zeros((tile, half), jnp.float32)
                    continue
                if k in (0, 1):
                    b = col - k + 2
                    right = jnp.concatenate([mine(k, b, own), mine(k, b, far)], axis=0)
                elif col not in (0, 1):
                    src = left_ref if k < 0 else right_ref
                    b = 2 * (k + 2) + (col + 2) if k < 0 else 2 * (k - 2) + (col - 2)
                    right = jnp.concatenate([src[b, own, :], src[b, far, :]], axis=0)
                else:
                    s = k - col + 2
                    right = jnp.concatenate([mine(col, s, own), other(col, s, own)], axis=1).T
                rh_ref[where] = right

    def one(x, y):
        return lax.dot_general(x, y, CONTRACT, precision=lax.Precision.HIGH, preferred_element_type=jnp.float32)

    for row in range(2):
        offsets = [o for o in range(5) if wanted(row + o - 2)]
        row_tiles = by_row[row]
        values = []
        for first in range(0, len(row_tiles), 2):
            chunk = range(first, min(first + 2, len(row_tiles)))
            used = [
                place_k
                for place_k, offset in enumerate(offsets)
                if any(abs(offset - row_tiles[place][1]) <= 2 for place in chunk)
            ]
            ks = slice(used[0] * tile, (used[-1] + 1) * tile)
            ns = slice(chunk[0] * half, (chunk[-1] + 1) * half)
            acc = one(lh_ref[row, :, ks], rh_ref[row, ks, ns])
            values += [acc[:, n * half : (n + 1) * half] for n in range(len(chunk))]
        for place, (index, slot) in enumerate(row_tiles):
            value = values[place]
            if mode == "own":
                out_ref[row, slot] = value
                continue
            if mode == "halo":
                value = value + partial_ref[row, slot]
            if odd:
                value = 2.0 * mine(row, slot) - value
            value = value * keep_ref[row, slot].astype(jnp.float32)
            if len(tiles) == len(ALL):
                out_ref[row, slot] = value
            else:
                out_ref[index] = value
    if quarters:
        for index, key in enumerate(QUARTERS):
            quarter_ref[index] = out_ref[tiles.index(key), own, :]


def band_call(tiles, odd, side, scale, keep, mine, other, halo=None, scaled=False, quarters=False, mode=None, partial=None):
    smem = pl.BlockSpec(memory_space=pltpu.SMEM)
    vmem = pl.BlockSpec(memory_space=pltpu.VMEM)
    if mode is None:
        mode = "plain" if halo is not None else "none"
    args = [side, scale, keep] + list(mine) + list(other)
    if halo is not None:
        args += list(halo)
    if partial is not None:
        args.append(partial)
    half = mine[0].shape[-1]
    tile = (mine[0].shape[-2], half)
    shape = (2, 5) + tile if len(tiles) == len(ALL) else (len(tiles),) + tile
    width = len(tiles) // 2
    count = {"own": 2, "halo": 3}.get(mode, 5)
    lefts = (2, tile[0], count * 2 * half)
    rights = (2, count * tile[0], width * half)
    out_shape = jax.ShapeDtypeStruct(shape, jnp.float32)
    if quarters:
        out_shape = (out_shape, jax.ShapeDtypeStruct((len(QUARTERS), half, half), jnp.float32))
    return pl.pallas_call(
        functools.partial(band_kernel, tiles, odd, len(mine), scaled, mode, quarters),
        out_shape=out_shape,
        in_specs=[smem, smem, smem] + [vmem] * (len(args) - 3),
        out_specs=(vmem, vmem) if quarters else vmem,
        scratch_shapes=[pltpu.VMEM(lefts, jnp.float32), pltpu.VMEM(rights, jnp.float32)],
    )(*args)


def block_kernel(pattern_ref, density_ref, out_ref):
    for index, (row, slot) in enumerate(DIAG):
        out_ref[index] = density_ref[row, slot] * pattern_ref[row, slot].astype(jnp.float32)


def first_block(pattern, density):
    return pl.pallas_call(
        block_kernel,
        out_shape=jax.ShapeDtypeStruct((len(DIAG),) + density.shape[2:], jnp.float32),
        in_specs=[pl.BlockSpec(memory_space=pltpu.SMEM), pl.BlockSpec(memory_space=pltpu.VMEM)],
        out_specs=pl.BlockSpec(memory_space=pltpu.VMEM),
    )(pattern, density)


def purify(density, pattern, truncation):
    side = lax.axis_index("help").astype(jnp.int32).reshape(1)
    halo = send_block(first_block(pattern, density))
    other = swap_help(density)
    diag, quarter = band_call(DIAG, False, side, pattern, truncation[0], [density], [other], scaled=True, quarters=True)
    next_halo = send_block(diag)
    quarter_other = swap_help(quarter)
    off = band_call(OFF, False, side, pattern, truncation[0], [density], [other], halo, scaled=True)
    off_other = swap_help(off)
    partial = band_call(ALL, True, side, pattern, truncation[1], [diag, off], [quarter_other], mode="own")
    return band_call(
        ALL, True, side, pattern, truncation[1], [diag, off], [quarter_other, off_other], next_halo, mode="halo", partial=partial
    )


def solution(mesh):
    return jax.shard_map(
        purify,
        mesh=mesh,
        in_specs=(P("rows", None, None, "help"), P("rows", None), P(None, "rows", None)),
        out_specs=P("rows", None, None, "help"),
        check_vma=False,
    )
```

```python
import functools

import jax
import jax.numpy as jnp
from jax import lax
from jax.experimental import pallas as pl
from jax.experimental.pallas import tpu as pltpu
from jax.sharding import PartitionSpec as P


DIAG = ((0, 2), (0, 3), (1, 1), (1, 2))
OFF = ((0, 0), (0, 1), (0, 4), (1, 0), (1, 3), (1, 4))
ALL = tuple((row, slot) for row in range(2) for slot in range(5))
CONTRACT = (((1,), (0,)), ((), ()))


def swap_help(value):
    return lax.ppermute(value, "help", [(0, 1), (1, 0)])


def send_block(block):
    count = lax.axis_size("rows")
    from_left = lax.ppermute(block, "rows", [(i, i + 1) for i in range(count - 1)])
    from_right = lax.ppermute(block, "rows", [(i + 1, i) for i in range(count - 1)])
    return from_left, from_right


def split(x):
    high = x.astype(jnp.bfloat16)
    return high, (x - high.astype(jnp.float32)).astype(jnp.bfloat16)


class Tiles:
    def __init__(self, refs, scale):
        self.refs = refs
        self.scale = scale

    def __call__(self, row, slot, rows=slice(None)):
        if len(self.refs) == 1:
            value = self.refs[0][row, slot, rows, :]
        elif (row, slot) in DIAG:
            value = self.refs[0][DIAG.index((row, slot)), rows, :]
        else:
            value = self.refs[1][OFF.index((row, slot)), rows, :]
        if self.scale is not None:
            value = value * self.scale[row, slot].astype(jnp.float32)
        return value


QUARTERS = ((0, 2), (0, 3), (1, 2))
FROM_QUARTER = {(0, 2): (0, False, (0, 2)), (0, 3): (1, False, (1, 1)), (1, 1): (1, True, (0, 3)), (1, 2): (2, False, (1, 2))}


class Rebuilt:
    def __init__(self, quarter_ref, off_ref, mine, side, own, far):
        self.quarter_ref, self.off_ref, self.mine = quarter_ref, off_ref, mine
        self.side, self.own, self.far = side, own, far

    def __call__(self, row, slot, rows=slice(None)):
        if (row, slot) not in DIAG:
            return self.off_ref[OFF.index((row, slot)), rows, :]
        index, flip, source = FROM_QUARTER[(row, slot)]
        quarter = self.quarter_ref[index]
        far_rows = quarter.T if flip else quarter
        own_rows = self.mine(source[0], source[1], self.far).T
        return jnp.where(
            self.side == 0,
            jnp.concatenate([own_rows, far_rows], axis=0),
            jnp.concatenate([far_rows, own_rows], axis=0),
        )


def band_kernel(tiles, odd, parts, scaled, mode, quarters, side_ref, scale_ref, keep_ref, *rest):
    mine = Tiles(rest[:parts], scale_ref if scaled else None)
    rest = rest[parts:]
    other_refs = rest[: len(rest) - 5 - (3 if mode == "halo" else (2 if mode == "plain" else 0)) - (1 if quarters else 0)]
    rest = rest[len(other_refs) :]
    if mode in ("plain", "halo"):
        left_ref, right_ref = rest[:2]
        rest = rest[2:]
    if mode == "halo":
        partial_ref = rest[0]
        rest = rest[1:]
    if quarters:
        out_ref, quarter_ref, lh_ref, ll_ref, rh_ref, rl_ref = rest
    else:
        out_ref, lh_ref, ll_ref, rh_ref, rl_ref = rest
    tile = lh_ref.shape[1]
    half = tile // 2
    side = side_ref[0]
    own = pl.ds(pl.multiple_of(side * half, half), half)
    far = pl.ds(pl.multiple_of((1 - side) * half, half), half)
    if other_refs[0].shape[-2] == half:
        other = Rebuilt(other_refs[0], other_refs[1] if len(other_refs) > 1 else None, mine, side, own, far)
    else:
        other = Tiles(other_refs, scale_ref if scaled else None)
    by_row = [[(index, slot) for index, (row, slot) in enumerate(tiles) if row == r] for r in range(2)]

    def wanted(k):
        if mode == "own":
            return k in (0, 1)
        if mode == "halo":
            return k not in (0, 1)
        return True

    for row in range(2):
        offsets = [o for o in range(5) if wanted(row + o - 2)]
        for place_k, offset in enumerate(offsets):
            high, low = split(jnp.concatenate([mine(row, offset), other(row, offset)], axis=1))
            lh_ref[row, :, place_k * tile : (place_k + 1) * tile] = high
            ll_ref[row, :, place_k * tile : (place_k + 1) * tile] = low
            k = row + offset - 2
            for place, (index, slot) in enumerate(by_row[row]):
                col = row + slot - 2
                where = (row, slice(place_k * tile, (place_k + 1) * tile), slice(place * half, (place + 1) * half))
                if abs(k - col) > 2:
                    rh_ref[where] = jnp.zeros((tile, half), jnp.bfloat16)
                    rl_ref[where] = jnp.zeros((tile, half), jnp.bfloat16)
                    continue
                if k in (0, 1):
                    b = col - k + 2
                    right = jnp.concatenate([mine(k, b, own), mine(k, b, far)], axis=0)
                elif col not in (0, 1):
                    src = left_ref if k < 0 else right_ref
                    b = 2 * (k + 2) + (col + 2) if k < 0 else 2 * (k - 2) + (col - 2)
                    right = jnp.concatenate([src[b, own, :], src[b, far, :]], axis=0)
                else:
                    s = k - col + 2
                    right = jnp.concatenate([mine(col, s, own), other(col, s, own)], axis=1).T
                high, low = split(right)
                rh_ref[where] = high
                rl_ref[where] = low

    def one(x, y):
        return lax.dot_general(x, y, CONTRACT, preferred_element_type=jnp.float32)

    for row in range(2):
        offsets = [o for o in range(5) if wanted(row + o - 2)]
        row_tiles = by_row[row]
        values = []
        for first in range(0, len(row_tiles), 2):
            chunk = range(first, min(first + 2, len(row_tiles)))
            used = [
                place_k
                for place_k, offset in enumerate(offsets)
                if any(abs(offset - row_tiles[place][1]) <= 2 for place in chunk)
            ]
            ks = slice(used[0] * tile, (used[-1] + 1) * tile)
            ns = slice(chunk[0] * half, (chunk[-1] + 1) * half)
            a_high = lh_ref[row, :, ks]
            b_high = rh_ref[row, ks, ns]
            acc = one(ll_ref[row, :, ks], b_high) + one(a_high, rl_ref[row, ks, ns]) + one(a_high, b_high)
            values += [acc[:, n * half : (n + 1) * half] for n in range(len(chunk))]
        for place, (index, slot) in enumerate(row_tiles):
            value = values[place]
            if mode == "own":
                out_ref[row, slot] = value
                continue
            if mode == "halo":
                value = value + partial_ref[row, slot]
            if odd:
                value = 2.0 * mine(row, slot) - value
            value = value * keep_ref[row, slot].astype(jnp.float32)
            if len(tiles) == len(ALL):
                out_ref[row, slot] = value
            else:
                out_ref[index] = value
    if quarters:
        for index, key in enumerate(QUARTERS):
            quarter_ref[index] = out_ref[tiles.index(key), own, :]


def band_call(tiles, odd, side, scale, keep, mine, other, halo=None, scaled=False, quarters=False, mode=None, partial=None):
    smem = pl.BlockSpec(memory_space=pltpu.SMEM)
    vmem = pl.BlockSpec(memory_space=pltpu.VMEM)
    if mode is None:
        mode = "plain" if halo is not None else "none"
    args = [side, scale, keep] + list(mine) + list(other)
    if halo is not None:
        args += list(halo)
    if partial is not None:
        args.append(partial)
    half = mine[0].shape[-1]
    tile = (mine[0].shape[-2], half)
    shape = (2, 5) + tile if len(tiles) == len(ALL) else (len(tiles),) + tile
    width = len(tiles) // 2
    count = {"own": 2, "halo": 3}.get(mode, 5)
    lefts = (2, tile[0], count * 2 * half)
    rights = (2, count * tile[0], width * half)
    out_shape = jax.ShapeDtypeStruct(shape, jnp.float32)
    if quarters:
        out_shape = (out_shape, jax.ShapeDtypeStruct((len(QUARTERS), half, half), jnp.float32))
    return pl.pallas_call(
        functools.partial(band_kernel, tiles, odd, len(mine), scaled, mode, quarters),
        out_shape=out_shape,
        in_specs=[smem, smem, smem] + [vmem] * (len(args) - 3),
        out_specs=(vmem, vmem) if quarters else vmem,
        scratch_shapes=[pltpu.VMEM(lefts, jnp.bfloat16)] * 2 + [pltpu.VMEM(rights, jnp.bfloat16)] * 2,
    )(*args)


def block_kernel(pattern_ref, *refs):
    out_ref = refs[-1]
    for index, (row, slot) in enumerate(DIAG):
        out_ref[index] = refs[index][0, 0] * pattern_ref[row, slot].astype(jnp.float32)


def first_block(pattern, density):
    tile = (1, 1) + density.shape[2:]
    specs = [pl.BlockSpec(tile, functools.partial(lambda r, s, i: (r, s, 0, 0), row, slot)) for row, slot in DIAG]
    return pl.pallas_call(
        block_kernel,
        grid=(1,),
        out_shape=jax.ShapeDtypeStruct((len(DIAG),) + density.shape[2:], jnp.float32),
        in_specs=[pl.BlockSpec(memory_space=pltpu.SMEM)] + specs,
        out_specs=pl.BlockSpec((len(DIAG),) + density.shape[2:], lambda i: (0, 0, 0)),
    )(pattern, *([density] * len(DIAG)))


def purify(density, pattern, truncation):
    side = lax.axis_index("help").astype(jnp.int32).reshape(1)
    halo = send_block(first_block(pattern, density))
    other = swap_help(density)
    diag, quarter = band_call(DIAG, False, side, pattern, truncation[0], [density], [other], scaled=True, quarters=True)
    next_halo = send_block(diag)
    quarter_other = swap_help(quarter)
    off = band_call(OFF, False, side, pattern, truncation[0], [density], [other], halo, scaled=True)
    off_other = swap_help(off)
    partial = band_call(ALL, True, side, pattern, truncation[1], [diag, off], [quarter_other], mode="own")
    return band_call(
        ALL, True, side, pattern, truncation[1], [diag, off], [quarter_other, off_other], next_halo, mode="halo", partial=partial
    )


def solution(mesh):
    return jax.shard_map(
        purify,
        mesh=mesh,
        in_specs=(P("rows", None, None, "help"), P("rows", None), P(None, "rows", None)),
        out_specs=P("rows", None, None, "help"),
        check_vma=False,
    )
```

```python
import functools

import jax
import jax.numpy as jnp
from jax import lax
from jax.experimental import pallas as pl
from jax.experimental.pallas import tpu as pltpu
from jax.sharding import PartitionSpec as P


DIAG = ((0, 2), (0, 3), (1, 1), (1, 2))
OFF = ((0, 0), (0, 1), (0, 4), (1, 0), (1, 3), (1, 4))
ALL = tuple((row, slot) for row in range(2) for slot in range(5))
CONTRACT = (((1,), (0,)), ((), ()))


def swap_help(value):
    return lax.ppermute(value, "help", [(0, 1), (1, 0)])


def send_block(block):
    count = lax.axis_size("rows")
    from_left = lax.ppermute(block, "rows", [(i, i + 1) for i in range(count - 1)])
    from_right = lax.ppermute(block, "rows", [(i + 1, i) for i in range(count - 1)])
    return from_left, from_right


def split(x):
    high = x.astype(jnp.bfloat16)
    return high, (x - high.astype(jnp.float32)).astype(jnp.bfloat16)


class Tiles:
    def __init__(self, refs, scale):
        self.refs = refs
        self.scale = scale

    def __call__(self, row, slot, rows=slice(None)):
        if len(self.refs) == 1:
            value = self.refs[0][row, slot, rows, :]
        elif (row, slot) in DIAG:
            value = self.refs[0][DIAG.index((row, slot)), rows, :]
        else:
            value = self.refs[1][OFF.index((row, slot)), rows, :]
        if self.scale is not None:
            value = value * self.scale[row, slot].astype(jnp.float32)
        return value


QUARTERS = ((0, 2), (0, 3), (1, 2))
FROM_QUARTER = {(0, 2): (0, False, (0, 2)), (0, 3): (1, False, (1, 1)), (1, 1): (1, True, (0, 3)), (1, 2): (2, False, (1, 2))}


class Rebuilt:
    def __init__(self, quarter_ref, off_ref, mine, side, own, far):
        self.quarter_ref, self.off_ref, self.mine = quarter_ref, off_ref, mine
        self.side, self.own, self.far = side, own, far

    def __call__(self, row, slot, rows=slice(None)):
        if (row, slot) not in DIAG:
            return self.off_ref[OFF.index((row, slot)), rows, :]
        index, flip, source = FROM_QUARTER[(row, slot)]
        quarter = self.quarter_ref[index]
        far_rows = quarter.T if flip else quarter
        own_rows = self.mine(source[0], source[1], self.far).T
        return jnp.where(
            self.side == 0,
            jnp.concatenate([own_rows, far_rows], axis=0),
            jnp.concatenate([far_rows, own_rows], axis=0),
        )


def band_kernel(tiles, odd, parts, scaled, mode, quarters, side_ref, scale_ref, keep_ref, *rest):
    mine = Tiles(rest[:parts], scale_ref if scaled else None)
    rest = rest[parts:]
    other_refs = rest[: len(rest) - 5 - (3 if mode == "halo" else (2 if mode == "plain" else 0)) - (1 if quarters else 0)]
    rest = rest[len(other_refs) :]
    if mode in ("plain", "halo"):
        left_ref, right_ref = rest[:2]
        rest = rest[2:]
    if mode == "halo":
        partial_ref = rest[0]
        rest = rest[1:]
    if quarters:
        out_ref, quarter_ref, lh_ref, ll_ref, rh_ref, rl_ref = rest
    else:
        out_ref, lh_ref, ll_ref, rh_ref, rl_ref = rest
    tile = lh_ref.shape[1]
    half = tile // 2
    side = side_ref[0]
    own = pl.ds(pl.multiple_of(side * half, half), half)
    far = pl.ds(pl.multiple_of((1 - side) * half, half), half)
    if other_refs[0].shape[-2] == half:
        other = Rebuilt(other_refs[0], other_refs[1] if len(other_refs) > 1 else None, mine, side, own, far)
    else:
        other = Tiles(other_refs, scale_ref if scaled else None)
    by_row = [[(index, slot) for index, (row, slot) in enumerate(tiles) if row == r] for r in range(2)]

    def wanted(k):
        if mode == "own":
            return k in (0, 1)
        if mode == "halo":
            return k not in (0, 1)
        return True

    for row in range(2):
        offsets = [o for o in range(5) if wanted(row + o - 2)]
        for place_k, offset in enumerate(offsets):
            high, low = split(jnp.concatenate([mine(row, offset), other(row, offset)], axis=1))
            lh_ref[row, :, place_k * tile : (place_k + 1) * tile] = high
            ll_ref[row, :, place_k * tile : (place_k + 1) * tile] = low
            k = row + offset - 2
            for place, (index, slot) in enumerate(by_row[row]):
                col = row + slot - 2
                where = (row, slice(place_k * tile, (place_k + 1) * tile), slice(place * half, (place + 1) * half))
                if abs(k - col) > 2:
                    first = place - place % 2
                    chunk = range(first, min(first + 2, len(by_row[row])))
                    used = [p for p, o in enumerate(offsets) if any(abs(o - by_row[row][q][1]) <= 2 for q in chunk)]
                    if not used[0] <= place_k <= used[-1]:
                        continue
                    rh_ref[where] = jnp.zeros((tile, half), jnp.bfloat16)
                    rl_ref[where] = jnp.zeros((tile, half), jnp.bfloat16)
                    continue
                if k in (0, 1):
                    b = col - k + 2
                    right = jnp.concatenate([mine(k, b, own), mine(k, b, far)], axis=0)
                elif col not in (0, 1):
                    src = left_ref if k < 0 else right_ref
                    b = 2 * (k + 2) + (col + 2) if k < 0 else 2 * (k - 2) + (col - 2)
                    right = jnp.concatenate([src[b, own, :], src[b, far, :]], axis=0)
                else:
                    s = k - col + 2
                    right = jnp.concatenate([mine(col, s, own), other(col, s, own)], axis=1).T
                high, low = split(right)
                rh_ref[where] = high
                rl_ref[where] = low

    def one(x, y):
        return lax.dot_general(x, y, CONTRACT, preferred_element_type=jnp.float32)

    for row in range(2):
        offsets = [o for o in range(5) if wanted(row + o - 2)]
        row_tiles = by_row[row]
        values = []
        for first in range(0, len(row_tiles), 2):
            chunk = range(first, min(first + 2, len(row_tiles)))
            used = [
                place_k
                for place_k, offset in enumerate(offsets)
                if any(abs(offset - row_tiles[place][1]) <= 2 for place in chunk)
            ]
            ks = slice(used[0] * tile, (used[-1] + 1) * tile)
            ns = slice(chunk[0] * half, (chunk[-1] + 1) * half)
            a_high = lh_ref[row, :, ks]
            b_high = rh_ref[row, ks, ns]
            acc = one(ll_ref[row, :, ks], b_high) + one(a_high, rl_ref[row, ks, ns]) + one(a_high, b_high)
            values += [acc[:, n * half : (n + 1) * half] for n in range(len(chunk))]
        for place, (index, slot) in enumerate(row_tiles):
            value = values[place]
            if mode == "own":
                out_ref[row, slot] = value
                continue
            if mode == "halo":
                value = value + partial_ref[row, slot]
            if odd:
                value = 2.0 * mine(row, slot) - value
            value = value * keep_ref[row, slot].astype(jnp.float32)
            if len(tiles) == len(ALL):
                out_ref[row, slot] = value
            else:
                out_ref[index] = value
    if quarters:
        for index, key in enumerate(QUARTERS):
            quarter_ref[index] = out_ref[tiles.index(key), own, :]


def band_call(tiles, odd, side, scale, keep, mine, other, halo=None, scaled=False, quarters=False, mode=None, partial=None):
    smem = pl.BlockSpec(memory_space=pltpu.SMEM)
    vmem = pl.BlockSpec(memory_space=pltpu.VMEM)
    if mode is None:
        mode = "plain" if halo is not None else "none"
    args = [side, scale, keep] + list(mine) + list(other)
    if halo is not None:
        args += list(halo)
    if partial is not None:
        args.append(partial)
    half = mine[0].shape[-1]
    tile = (mine[0].shape[-2], half)
    shape = (2, 5) + tile if len(tiles) == len(ALL) else (len(tiles),) + tile
    width = len(tiles) // 2
    count = {"own": 2, "halo": 3}.get(mode, 5)
    lefts = (2, tile[0], count * 2 * half)
    rights = (2, count * tile[0], width * half)
    out_shape = jax.ShapeDtypeStruct(shape, jnp.float32)
    if quarters:
        out_shape = (out_shape, jax.ShapeDtypeStruct((len(QUARTERS), half, half), jnp.float32))
    return pl.pallas_call(
        functools.partial(band_kernel, tiles, odd, len(mine), scaled, mode, quarters),
        out_shape=out_shape,
        in_specs=[smem, smem, smem] + [vmem] * (len(args) - 3),
        out_specs=(vmem, vmem) if quarters else vmem,
        scratch_shapes=[pltpu.VMEM(lefts, jnp.bfloat16)] * 2 + [pltpu.VMEM(rights, jnp.bfloat16)] * 2,
    )(*args)


def block_kernel(pattern_ref, *refs):
    out_ref = refs[-1]
    for index, (row, slot) in enumerate(DIAG):
        out_ref[index] = refs[index][0, 0] * pattern_ref[row, slot].astype(jnp.float32)


def first_block(pattern, density):
    tile = (1, 1) + density.shape[2:]
    specs = [pl.BlockSpec(tile, functools.partial(lambda r, s, i: (r, s, 0, 0), row, slot)) for row, slot in DIAG]
    return pl.pallas_call(
        block_kernel,
        grid=(1,),
        out_shape=jax.ShapeDtypeStruct((len(DIAG),) + density.shape[2:], jnp.float32),
        in_specs=[pl.BlockSpec(memory_space=pltpu.SMEM)] + specs,
        out_specs=pl.BlockSpec((len(DIAG),) + density.shape[2:], lambda i: (0, 0, 0)),
    )(pattern, *([density] * len(DIAG)))


def purify(density, pattern, truncation):
    side = lax.axis_index("help").astype(jnp.int32).reshape(1)
    halo = send_block(first_block(pattern, density))
    other = swap_help(density)
    diag, quarter = band_call(DIAG, False, side, pattern, truncation[0], [density], [other], scaled=True, quarters=True)
    next_halo = send_block(diag)
    quarter_other = swap_help(quarter)
    off = band_call(OFF, False, side, pattern, truncation[0], [density], [other], halo, scaled=True)
    off_other = swap_help(off)
    partial = band_call(ALL, True, side, pattern, truncation[1], [diag, off], [quarter_other], mode="own")
    return band_call(
        ALL, True, side, pattern, truncation[1], [diag, off], [quarter_other, off_other], next_halo, mode="halo", partial=partial
    )


def solution(mesh):
    return jax.shard_map(
        purify,
        mesh=mesh,
        in_specs=(P("rows", None, None, "help"), P("rows", None), P(None, "rows", None)),
        out_specs=P("rows", None, None, "help"),
        check_vma=False,
    )
```
